256 devices in a mesh: req: 64 (over z, x, core), kv: 4 (over y).
Axes of the slice: x: 4, y: 4, z: 8, core: 2. Of those that a mesh axis runs over, the one named last changes fastest.
Arguments:
- residual_in: bfloat16 [128, 2560], P('req', 'kv'), may hold values from -8 to 8
- queries: bfloat16 [128, 2560], P('req', 'kv'), may hold values from -480 to 480
- fresh_token_keys: bfloat16 [128, 512], P('req', 'kv'), may hold values from -6 to 6
- fresh_token_values: bfloat16 [128, 512], P('req', 'kv'), may hold values from -6 to 6
- cached_key_slots: bfloat16 [128, 4096, 512], P('req', None, 'kv'), may hold values from -6 to 6
- cached_value_slots: bfloat16 [128, 4096, 512], P('req', None, 'kv'), may hold values from -6 to 6
- lengths: int32 [128], replicated, may hold values from 1 to 4096, as said below
- slot_order: int32 [128], replicated, may hold values from 0 to 127, as said below
- out_proj: bfloat16 [2560, 2560], P('kv'), may hold values from -0.5 to 0.5
- norm_gain: bfloat16 [2560], P('kv'), may hold values from 0.5 to 1.5
- expert_ids: int32 [128, 6], replicated, may hold values from 0 to 63, all different within a row; in each aligned block of 128 rows (0 to 127, 128 to 255, ...) at most 24 rows name the same one
- gate_values: float32 [128, 6], replicated, may hold values from 0.1 to 0.5
- gate_proj: bfloat16 [64, 2560, 1536], P('req', None, 'kv'), may hold values from -0.125 to 0.125
- up_proj: bfloat16 [64, 2560, 1536], P('req', None, 'kv'), may hold values from -0.125 to 0.125
- down_proj: bfloat16 [64, 1536, 2560], P('req', 'kv'), may hold values from -0.15625 to 0.15625
Outputs:
- layer_out: bfloat16 [128, 2560], P('req', 'kv')
The draws below stay inside these ranges and needn't reach their ends.
Inputs may be any that keep to these rules, and one draw needn't show every extreme that they name: `lengths`: each request's count of cached positions; some request has exactly 4096. A permutation of the requests: slot s serves request slot_order[s], and cached_key_slots[s], cached_value_slots[s] hold that request's cache. Requests sorted by decreasing length are dealt to the 64 groups of 2 consecutive slots, one round forward, the next backward. `expert_ids`: each token names 6 different experts; no expert is named by more than 24 tokens, a bound that some block reaches.
All inputs are finite; a program needn't handle non-finite values.
Results may differ from the reference program's by a relative error of at most 0.012.
Values may be sent and summed in bfloat16 or wider, within the bound.
No kernel may reach another device: no remote copies, remote signals or barrier semaphores. Data moves between devices by JAX's collectives and lax.ppermute only.
A program may use at most 64 MiB of HBM per device.

```python
import math
import jax
import jax.numpy as jnp
import numpy as np
from jax import lax

D = 2560
QUERY_HEADS = 20
KEY_VALUE_HEADS = 4
HEAD_SIZE = 128
FE = 1536
TOPK = 6
REQ_DEV = 2
LONGEST_LENGTH = 4096
REQUEST_TOTAL = 128
NE = 64
CAPE = 24


def length_table(key):
    base_key = jax.random.fold_in(key, 11)
    first_key = jax.random.fold_in(base_key, 1)
    second_key = jax.random.fold_in(base_key, 2)
    third_key = jax.random.fold_in(base_key, 3)
    ceiling = jax.random.randint(first_key, (REQUEST_TOTAL,), 1, LONGEST_LENGTH + 1)
    raw_len = jax.random.randint(second_key, (REQUEST_TOTAL,), 0, LONGEST_LENGTH)
    lens_all = 1 + raw_len % ceiling
    spot_row = jax.random.randint(third_key, (), 0, REQUEST_TOTAL)
    return jnp.where(jnp.arange(REQUEST_TOTAL) == spot_row, LONGEST_LENGTH, lens_all).astype(jnp.int32)


def draw_lengths(key, part):
    return length_table(key)


def draw_slot_order(key, part):
    lens_all = length_table(key)
    ranking = lens_all * REQUEST_TOTAL + jnp.arange(REQUEST_TOTAL, dtype=jnp.int32)
    sorted_req = jnp.argsort(-ranking, stable=True).astype(jnp.int32)
    groups = REQUEST_TOTAL // REQ_DEV
    slot_ids = jnp.arange(REQUEST_TOTAL, dtype=jnp.int32)
    group_id = slot_ids // REQ_DEV
    round_id = slot_ids % REQ_DEV
    rank_pos = round_id * groups + jnp.where(round_id % 2 == 0, group_id, groups - 1 - group_id)
    return sorted_req[rank_pos].astype(jnp.int32)


def draw_queries(key, part):
    values = jax.random.truncated_normal(jax.random.fold_in(key, 3), -6.0, 6.0, (REQUEST_TOTAL, QUERY_HEADS, HEAD_SIZE), jnp.float32) * 2.0
    return values.reshape(REQUEST_TOTAL, QUERY_HEADS * HEAD_SIZE).astype(jnp.bfloat16)


def draw_residual_in(key, part):
    base = jax.random.truncated_normal(jax.random.fold_in(key, 21), -3.0, 3.0, (REQUEST_TOTAL, D), jnp.float32)
    place = jnp.arange(D, dtype=jnp.float32) / (D - 1)
    column_scale = 0.3 * jnp.exp(place * math.log(5.0))
    values = base * column_scale[None, :]
    return jnp.clip(values, -8.0, 8.0).astype(jnp.bfloat16)


def level_of(key, dims, split, low, top_value):
    gain, own = 1.0, jax.random.fold_in(key, 6)
    for position, shards_of in split:
        heights = jnp.exp(jax.random.uniform(jax.random.fold_in(own, position), (shards_of,), jnp.float32, low / len(split), top_value / len(split)))
        gain = gain * jnp.repeat(heights, dims[position] // shards_of).reshape([-1 if axis == position else 1 for axis in range(len(dims))])
    return gain


def routed_block(key, own, number, rows, count, top, bound, lean):
    order = jax.random.permutation(key, count)
    crowded, common = load_shares(count, rows * top, bound, lean, True), load_shares(count, rows * top, bound, lean, False)
    places = jnp.arange(count)

    def named(tallies, offset_by):
        used = int((tallies > 0).sum())
        fixed = max(1, used // 4)
        moved = fixed + (places - fixed + offset_by * (used - fixed)) % max(1, count - fixed)
        return jnp.zeros((count,), jnp.int32).at[order[jnp.where(places < fixed, places, moved)]].set(jnp.asarray(tallies, jnp.int32))

    tallies = jnp.where(number % 4 == 0, named(crowded, number // 4), named(common, number - number // 4 - 1))
    mixed = jax.random.permutation(jax.random.fold_in(own, 3), count)
    source_of, sink = mixed[0:count // 2 * 2:2], mixed[1:count // 2 * 2:2]
    margin = jnp.minimum(tallies[source_of] - 1, bound - tallies[sink]) // 2
    margin = jnp.where((source_of == order[0]) | (sink == order[0]) | (tallies[sink] == 0), 0, jnp.maximum(margin, 0))
    moved = jax.random.randint(jax.random.fold_in(own, 4), (count // 2,), 0, 1 << 20) % (margin + 1)
    tallies = tallies.at[source_of].add(-moved).at[sink].add(moved)
    labels = jnp.searchsorted(jnp.cumsum(tallies), jnp.arange(rows * top), side="right").astype(jnp.int32)
    table = labels.reshape(top, rows).T
    table = table[jax.random.permutation(jax.random.fold_in(own, 1), rows)]
    offset_by = jax.random.randint(jax.random.fold_in(own, 2), (rows, 1), 0, top)
    return jnp.take_along_axis(table, (jnp.arange(top)[None, :] + offset_by) % top, axis=1)


def load_shares(number_of, total, bound, skew, full):
    weights = [(1 << 20) // math.isqrt(rank ** skew) + 1 for rank in range(1, number_of + 1)]
    largest = bound if full else min(bound, max(-(-total // number_of), total * weights[0] // sum(weights)))
    least = 1 if total - largest >= number_of - 1 else 0
    holding, surplus = [largest] + [least] * (number_of - 1), total - largest - least * (number_of - 1)
    while surplus > 0:
        candidates = [i for i in range(1, number_of) if holding[i] < largest] or [i for i in range(1, number_of) if holding[i] < bound]
        whole, remaining = sum([weights[i] for i in candidates]), surplus
        for i in candidates:
            extra = min(bound - holding[i], max(1, remaining * weights[i] // whole), surplus)
            holding[i] = holding[i] + extra
            surplus = surplus - extra
    return np.array(holding)


def scatter_about(rng, dims, width, bound, cuts=(), held_as=jnp.bfloat16):
    factor_of = level_of(rng, dims, cuts, -0.22, 0.18) if cuts else 1.0
    result = jax.random.normal(rng, dims, jnp.float32) * width * factor_of
    return jnp.minimum(jnp.maximum(result, -bound), bound).astype(held_as)


def setup_inputs(seed: int = 0) -> dict:
    key_of = jax.random.split(jax.random.key(seed), 16)
    residual_in = draw_residual_in(jax.random.fold_in(key_of[15], 71), 0)
    queries = draw_queries(jax.random.fold_in(key_of[15], 71), 0)
    fresh_token_keys = scatter_about(key_of[2], (REQUEST_TOTAL, KEY_VALUE_HEADS * HEAD_SIZE), 1.0, 6.0, ((0, 64), (1, 4)))
    fresh_token_values = scatter_about(key_of[3], (REQUEST_TOTAL, KEY_VALUE_HEADS * HEAD_SIZE), 1.0, 6.0, ((0, 64), (1, 4)))
    cached_key_slots = scatter_about(key_of[4], (REQUEST_TOTAL, LONGEST_LENGTH, KEY_VALUE_HEADS * HEAD_SIZE), 1.0, 6.0, ((0, 64), (2, 4)))
    cached_value_slots = scatter_about(key_of[5], (REQUEST_TOTAL, LONGEST_LENGTH, KEY_VALUE_HEADS * HEAD_SIZE), 1.0, 6.0, ((0, 64), (2, 4)))
    lengths = draw_lengths(jax.random.fold_in(key_of[15], 71), 0)
    slot_order = draw_slot_order(jax.random.fold_in(key_of[15], 71), 0)
    out_proj = scatter_about(key_of[8], (QUERY_HEADS * HEAD_SIZE, D), HEAD_SIZE ** -0.5, 0.5, ((0, 4),))
    norm_gain = jnp.clip(1.0 + 0.1 * jax.random.normal(key_of[9], (D,), jnp.float32), 0.5, 1.5).astype(jnp.bfloat16)
    expert_ids_keys = jax.random.split(jax.random.fold_in(key_of[10], 1), REQUEST_TOTAL // REQUEST_TOTAL)
    expert_ids_turns = jax.random.permutation(jax.random.fold_in(key_of[10], 3), REQUEST_TOTAL // REQUEST_TOTAL)
    expert_ids = jax.vmap(lambda own, number: routed_block(jax.random.fold_in(key_of[10], 2), own, number, REQUEST_TOTAL, NE, TOPK, CAPE, 1))(expert_ids_keys, expert_ids_turns).reshape((REQUEST_TOTAL, TOPK))
    gate_values = jnp.clip(jax.random.uniform(key_of[11], (REQUEST_TOTAL, TOPK), jnp.float32, 0.1, 0.5), 0.1, 0.5)
    gate_proj = scatter_about(key_of[12], (NE, D, FE), D ** -0.5, 0.125, ((0, 64), (2, 4)))
    up_proj = scatter_about(key_of[13], (NE, D, FE), D ** -0.5, 0.125, ((0, 64), (2, 4)))
    down_proj = scatter_about(key_of[14], (NE, FE, D), FE ** -0.5, 0.15625, ((0, 64), (1, 4)))
    return dict(residual_in=residual_in, queries=queries, fresh_token_keys=fresh_token_keys, fresh_token_values=fresh_token_values, cached_key_slots=cached_key_slots, cached_value_slots=cached_value_slots, lengths=lengths, slot_order=slot_order, out_proj=out_proj, norm_gain=norm_gain, expert_ids=expert_ids, gate_values=gate_values, gate_proj=gate_proj, up_proj=up_proj, down_proj=down_proj)


def attend_slot(rows_per_head, request_key, request_value, gathered_keys, gathered_values, length):
    rows_per_head = rows_per_head.reshape(KEY_VALUE_HEADS, QUERY_HEADS // KEY_VALUE_HEADS, HEAD_SIZE).astype(jnp.float32)
    gathered_keys = gathered_keys.reshape(LONGEST_LENGTH, KEY_VALUE_HEADS, HEAD_SIZE).astype(jnp.float32)
    gathered_values = gathered_values.reshape(LONGEST_LENGTH, KEY_VALUE_HEADS, HEAD_SIZE).astype(jnp.float32)
    self_key_row = request_key.reshape(KEY_VALUE_HEADS, HEAD_SIZE).astype(jnp.float32)
    self_value_row = request_value.reshape(KEY_VALUE_HEADS, HEAD_SIZE).astype(jnp.float32)
    inv_root = 1.0 / math.sqrt(HEAD_SIZE)
    scores = jnp.einsum('gqd,lgd->gql', rows_per_head, gathered_keys) * inv_root
    positions = jnp.arange(LONGEST_LENGTH)
    scores = jnp.where((positions < length)[None, None, :], scores, -1e+30)
    own_score = jnp.einsum('gqd,gd->gq', rows_per_head, self_key_row) * inv_root
    highest = jnp.maximum(lax.optimization_barrier(jnp.max(scores, axis=2)), own_score)
    weights = jnp.exp(scores - highest[:, :, None])
    own_weight = jnp.exp(own_score - highest)
    totals = lax.optimization_barrier(jnp.sum(weights, axis=2)) + own_weight
    weights_low = lax.optimization_barrier(weights.astype(jnp.bfloat16)).astype(jnp.float32)
    own_low = lax.optimization_barrier(own_weight.astype(jnp.bfloat16)).astype(jnp.float32)
    numerator = jnp.einsum('gql,lgd->gqd', weights_low, gathered_values) + own_low[:, :, None] * self_value_row[:, None, :]
    return (numerator / totals[:, :, None]).astype(jnp.bfloat16).reshape(QUERY_HEADS * HEAD_SIZE)

def attend_pack(packed):
    return attend_slot(*packed)

def reference(residual_in, queries, fresh_token_keys, fresh_token_values, cached_key_slots, cached_value_slots, lengths, slot_order, out_proj, norm_gain, expert_ids, gate_values, gate_proj, up_proj, down_proj):
    slot_len = lengths[slot_order]
    attended = lax.map(attend_pack, (queries[slot_order], fresh_token_keys[slot_order], fresh_token_values[slot_order], cached_key_slots, cached_value_slots, slot_len))
    projected = jnp.dot(attended, out_proj, preferred_element_type=jnp.float32)
    by_request = jnp.zeros((REQUEST_TOTAL, D), jnp.float32).at[slot_order].set(projected)
    hidden = residual_in.astype(jnp.float32) + by_request
    mean_sq = lax.optimization_barrier(jnp.sum(hidden * hidden, axis=1)) / D
    normed = (hidden * lax.rsqrt(mean_sq + 1e-06)[:, None] * norm_gain.astype(jnp.float32)).astype(jnp.bfloat16)
    flat_ids = expert_ids.reshape(-1)
    flat_gates = gate_values.reshape(-1)

    def expert_step(mixture, expert):
        picked = jnp.argsort((flat_ids != expert).astype(jnp.int32), stable=True)[:CAPE].astype(jnp.int32)
        chosen = flat_ids[picked] == expert
        token_idx = (picked // TOPK).astype(jnp.int32)
        row_block = normed[token_idx]
        gate_h = jnp.dot(row_block, gate_proj[expert], preferred_element_type=jnp.float32)
        up_h = jnp.dot(row_block, up_proj[expert], preferred_element_type=jnp.float32)
        inner_act = (jax.nn.silu(gate_h) * up_h).astype(jnp.bfloat16)
        outputs = jnp.dot(inner_act, down_proj[expert], preferred_element_type=jnp.float32)
        token_gate = jnp.where(chosen, flat_gates[picked], jnp.zeros_like(flat_gates[picked]))
        return (mixture.at[token_idx].add(outputs * token_gate[:, None]), None)
    mixture, _ = lax.scan(expert_step, jnp.zeros((REQUEST_TOTAL, D), jnp.float32), jnp.arange(NE, dtype=jnp.int32))
    return (hidden + mixture).astype(jnp.bfloat16)
```

```python
import math

import jax
import jax.numpy as jnp
from jax import lax
from jax.sharding import PartitionSpec as P

COMBINE = "a2a"


def per_device(
    residual_in,
    queries,
    fresh_token_keys,
    fresh_token_values,
    cached_key_slots,
    cached_value_slots,
    lengths,
    slot_order,
    out_proj,
    norm_gain,
    expert_ids,
    gate_values,
    gate_proj,
    up_proj,
    down_proj,
):
    req_count = lax.axis_size("req")
    kv_count = lax.axis_size("kv")
    req_index = lax.axis_index("req")
    kv_index = lax.axis_index("kv")
    per_dev = residual_in.shape[0]
    head_dim = fresh_token_keys.shape[1]
    col_count = residual_in.shape[1]
    total_reqs = lengths.shape[0]
    model_width = out_proj.shape[1]
    q_width = queries.shape[1]

    packed = jnp.concatenate([queries, fresh_token_keys, fresh_token_values, residual_in], axis=1)
    all_packed = lax.all_gather(packed, "req", axis=0, tiled=True)
    served = lax.dynamic_slice_in_dim(slot_order, req_index * per_dev, per_dev)
    mine = all_packed[served]
    query_rows = mine[:, :q_width].reshape(per_dev, -1, head_dim)
    self_key_row = mine[:, q_width:q_width + head_dim]
    self_value_row = mine[:, q_width + head_dim:q_width + 2 * head_dim]
    residual_rows = mine[:, q_width + 2 * head_dim:]
    live_len = lengths[served]

    inv_root = 1.0 / math.sqrt(head_dim)
    scores = (
        jnp.einsum("rqd,rld->rql", query_rows, cached_key_slots, preferred_element_type=jnp.float32)
        * inv_root
    )
    positions = jnp.arange(cached_key_slots.shape[1])
    scores = jnp.where((positions[None, :] < live_len[:, None])[:, None, :], scores, -1e30)
    own_score = (
        jnp.einsum("rqd,rd->rq", query_rows, self_key_row, preferred_element_type=jnp.float32)
        * inv_root
    )
    highest = jnp.maximum(jnp.max(scores, axis=2), own_score)
    weights = jnp.exp(scores - highest[:, :, None])
    own_weight = jnp.exp(own_score - highest)
    totals = jnp.sum(weights, axis=2) + own_weight
    numerator = jnp.einsum(
        "rql,rld->rqd",
        weights.astype(jnp.bfloat16),
        cached_value_slots,
        preferred_element_type=jnp.float32,
    )
    own_low = lax.optimization_barrier(own_weight.astype(jnp.bfloat16)).astype(jnp.float32)
    numerator = numerator + own_low[:, :, None] * self_value_row.astype(jnp.float32)[:, None, :]
    attended = (numerator / totals[:, :, None]).astype(jnp.bfloat16).reshape(per_dev, -1)
    projected = jnp.dot(attended, out_proj, preferred_element_type=jnp.float32)

    col_start = kv_index * col_count
    own_cols = jnp.concatenate(
        [residual_rows.astype(jnp.float32), norm_gain.astype(jnp.float32)[None, :]], axis=0
    )
    summed_in = jnp.concatenate(
        [projected, jnp.zeros((1, model_width), jnp.float32)], axis=0
    ) + lax.dynamic_update_slice(
        jnp.zeros((per_dev + 1, model_width), jnp.float32), own_cols, (0, col_start)
    )
    summed = lax.psum(summed_in, "kv")
    hidden = summed[:per_dev]
    gain = summed[per_dev]
    squares = jnp.sum(hidden * hidden, axis=1)
    normed = (hidden * lax.rsqrt(squares / model_width + 1e-06)[:, None] * gain).astype(
        jnp.bfloat16
    )
    by_slot = lax.all_gather(normed, "req", axis=0, tiled=True)
    slot_of = jnp.zeros((total_reqs,), jnp.int32).at[slot_order].set(
        jnp.arange(total_reqs, dtype=jnp.int32)
    )

    local_count = gate_proj.shape[0]
    capacity = min(2 * total_reqs * expert_ids.shape[1] // (local_count * req_count), total_reqs)
    expert = req_index * local_count + 0
    named_here = expert_ids == expert
    token_gate = jnp.sum(jnp.where(named_here, gate_values, 0.0), axis=1)
    uses_expert = jnp.any(named_here, axis=1)
    picked = jnp.nonzero(uses_expert, size=capacity, fill_value=0)[0].astype(jnp.int32)
    valid_rows = jnp.arange(capacity) < jnp.sum(uses_expert.astype(jnp.int32))
    row_block = by_slot[slot_of[picked]]
    gate_h = jnp.dot(row_block, gate_proj[0], preferred_element_type=jnp.float32)
    up_h = jnp.dot(row_block, up_proj[0], preferred_element_type=jnp.float32)
    inner_act = (jax.nn.silu(gate_h) * up_h).astype(jnp.bfloat16)
    outputs = jnp.dot(inner_act, down_proj[0], preferred_element_type=jnp.float32)
    row_gate = jnp.where(valid_rows, token_gate[picked], 0.0)
    weighted = outputs * row_gate[:, None]
    weighted = lax.psum_scatter(weighted, "kv", scatter_dimension=1, tiled=True)

    own_hidden = lax.dynamic_slice_in_dim(hidden, col_start, col_count, axis=1)
    combined = (
        jnp.zeros((total_reqs, col_count), jnp.float32)
        .at[picked]
        .add(weighted)
        .at[served]
        .add(own_hidden)
    )
    if COMBINE == "rs":
        layer_rows = lax.psum_scatter(combined, "req", scatter_dimension=0, tiled=True)
    else:
        layer_rows = jnp.sum(
            lax.all_to_all(
                combined.reshape(req_count, per_dev, col_count), "req", 0, 0, tiled=False
            ),
            axis=0,
        )
    return layer_rows.astype(jnp.bfloat16)


def solution(mesh):
    in_specs = (
        P("req", "kv"),
        P("req", "kv"),
        P("req", "kv"),
        P("req", "kv"),
        P("req", None, "kv"),
        P("req", None, "kv"),
        P(),
        P(),
        P("kv", None),
        P("kv"),
        P(),
        P(),
        P("req", None, "kv"),
        P("req", None, "kv"),
        P("req", "kv", None),
    )
    out_specs = P("req", "kv")
    return jax.shard_map(
        per_device, mesh=mesh, in_specs=in_specs, out_specs=out_specs, check_vma=False
    )
```

```python
import math

import jax
import jax.numpy as jnp
from jax import lax
from jax.sharding import PartitionSpec as P


def per_device(
    residual_in,
    queries,
    fresh_token_keys,
    fresh_token_values,
    cached_key_slots,
    cached_value_slots,
    lengths,
    slot_order,
    out_proj,
    norm_gain,
    expert_ids,
    gate_values,
    gate_proj,
    up_proj,
    down_proj,
):
    req_count = lax.axis_size("req")
    kv_count = lax.axis_size("kv")
    req_index = lax.axis_index("req")
    kv_index = lax.axis_index("kv")
    per_dev = residual_in.shape[0]
    head_dim = fresh_token_keys.shape[1]
    col_count = residual_in.shape[1]
    total_reqs = lengths.shape[0]
    model_width = out_proj.shape[1]
    q_width = queries.shape[1]

    packed = jnp.concatenate([queries, fresh_token_keys, fresh_token_values, residual_in], axis=1)
    slot_of = jnp.zeros((total_reqs,), jnp.int32).at[slot_order].set(
        jnp.arange(total_reqs, dtype=jnp.int32)
    )
    home_slots = lax.dynamic_slice_in_dim(slot_of, req_index * per_dev, per_dev)
    to_slots = jnp.zeros((total_reqs, packed.shape[1]), packed.dtype).at[home_slots].set(packed)
    from_homes = lax.all_to_all(
        to_slots.reshape(req_count, per_dev, -1), "req", 0, 0, tiled=False
    )
    served = lax.dynamic_slice_in_dim(slot_order, req_index * per_dev, per_dev)
    mine = from_homes[served // per_dev, jnp.arange(per_dev)]
    query_rows = mine[:, :q_width].reshape(per_dev, -1, head_dim)
    self_key_row = mine[:, q_width:q_width + head_dim]
    self_value_row = mine[:, q_width + head_dim:q_width + 2 * head_dim]
    residual_rows = mine[:, q_width + 2 * head_dim:]
    live_len = lengths[served]

    inv_root = 1.0 / math.sqrt(head_dim)
    scores = (
        jnp.einsum("rqd,rld->rql", query_rows, cached_key_slots, preferred_element_type=jnp.float32)
        * inv_root
    )
    positions = jnp.arange(cached_key_slots.shape[1])
    scores = jnp.where((positions[None, :] < live_len[:, None])[:, None, :], scores, -1e30)
    own_score = (
        jnp.einsum("rqd,rd->rq", query_rows, self_key_row, preferred_element_type=jnp.float32)
        * inv_root
    )
    highest = jnp.maximum(jnp.max(scores, axis=2), own_score)
    weights = jnp.exp(scores - highest[:, :, None])
    own_weight = jnp.exp(own_score - highest)
    totals = jnp.sum(weights, axis=2) + own_weight
    numerator = jnp.einsum(
        "rql,rld->rqd",
        weights.astype(jnp.bfloat16),
        cached_value_slots,
        preferred_element_type=jnp.float32,
    )
    own_low = lax.optimization_barrier(own_weight.astype(jnp.bfloat16)).astype(jnp.float32)
    numerator = numerator + own_low[:, :, None] * self_value_row.astype(jnp.float32)[:, None, :]
    attended = (numerator / totals[:, :, None]).astype(jnp.bfloat16).reshape(per_dev, -1)
    projected = jnp.dot(attended, out_proj, preferred_element_type=jnp.float32)

    col_start = kv_index * col_count
    own_cols = jnp.concatenate(
        [residual_rows.astype(jnp.float32), norm_gain.astype(jnp.float32)[None, :]], axis=0
    )
    summed_in = jnp.concatenate(
        [projected, jnp.zeros((1, model_width), jnp.float32)], axis=0
    ) + lax.dynamic_update_slice(
        jnp.zeros((per_dev + 1, model_width), jnp.float32), own_cols, (0, col_start)
    )
    summed = summed_in
    step = 1
    while step < kv_count:
        summed = summed + lax.ppermute(
            summed, "kv", [(i, i ^ step) for i in range(kv_count)]
        )
        step *= 2
    hidden = summed[:per_dev]
    gain = summed[per_dev]
    squares = jnp.sum(hidden * hidden, axis=1)
    normed = (hidden * lax.rsqrt(squares / model_width + 1e-06)[:, None] * gain).astype(
        jnp.bfloat16
    )
    local_count = gate_proj.shape[0]
    served_ids = expert_ids[served] // local_count
    wanted = jnp.any(
        served_ids[None, :, :] == jnp.arange(req_count, dtype=jnp.int32)[:, None, None], axis=2
    )
    to_experts = jnp.where(wanted[:, :, None], normed[None, :, :], jnp.zeros_like(normed)[None])
    by_slot = lax.all_to_all(to_experts, "req", 0, 0, tiled=False).reshape(total_reqs, -1)

    capacity = min(2 * total_reqs * expert_ids.shape[1] // (local_count * req_count), total_reqs)
    expert = req_index * local_count + 0
    named_here = expert_ids == expert
    token_gate = jnp.sum(jnp.where(named_here, gate_values, 0.0), axis=1)
    uses_expert = jnp.any(named_here, axis=1)
    picked = jnp.nonzero(uses_expert, size=capacity, fill_value=0)[0].astype(jnp.int32)
    valid_rows = jnp.arange(capacity) < jnp.sum(uses_expert.astype(jnp.int32))
    row_block = by_slot[slot_of[picked]]
    gate_h = jnp.dot(row_block, gate_proj[0], preferred_element_type=jnp.float32)
    up_h = jnp.dot(row_block, up_proj[0], preferred_element_type=jnp.float32)
    inner_act = (jax.nn.silu(gate_h) * up_h).astype(jnp.bfloat16)
    outputs = jnp.dot(inner_act, down_proj[0], preferred_element_type=jnp.float32)
    row_gate = jnp.where(valid_rows, token_gate[picked], 0.0)
    weighted = outputs * row_gate[:, None]
    weighted = jnp.sum(
        lax.all_to_all(
            weighted.reshape(capacity, kv_count, col_count).transpose(1, 0, 2),
            "kv",
            0,
            0,
            tiled=False,
        ),
        axis=0,
    )

    own_hidden = lax.dynamic_slice_in_dim(hidden, col_start, col_count, axis=1)
    combined = (
        jnp.zeros((total_reqs, col_count), jnp.float32)
        .at[picked]
        .add(weighted)
        .at[served]
        .add(own_hidden)
    )
    layer_rows = jnp.sum(
        lax.all_to_all(combined.reshape(req_count, per_dev, col_count), "req", 0, 0, tiled=False),
        axis=0,
    )
    return layer_rows.astype(jnp.bfloat16)


def solution(mesh):
    in_specs = (
        P("req", "kv"),
        P("req", "kv"),
        P("req", "kv"),
        P("req", "kv"),
        P("req", None, "kv"),
        P("req", None, "kv"),
        P(),
        P(),
        P("kv", None),
        P("kv"),
        P(),
        P(),
        P("req", None, "kv"),
        P("req", None, "kv"),
        P("req", "kv", None),
    )
    out_specs = P("req", "kv")
    return jax.shard_map(
        per_device, mesh=mesh, in_specs=in_specs, out_specs=out_specs, check_vma=False
    )
```

```python
import math

import jax
import jax.numpy as jnp
from jax import lax
from jax.sharding import PartitionSpec as P


def per_device(
    residual_in,
    queries,
    fresh_token_keys,
    fresh_token_values,
    cached_key_slots,
    cached_value_slots,
    lengths,
    slot_order,
    out_proj,
    norm_gain,
    expert_ids,
    gate_values,
    gate_proj,
    up_proj,
    down_proj,
):
    req_count = lax.axis_size("req")
    kv_count = lax.axis_size("kv")
    req_index = lax.axis_index("req")
    kv_index = lax.axis_index("kv")
    per_dev = residual_in.shape[0]
    head_dim = fresh_token_keys.shape[1]
    col_count = residual_in.shape[1]
    total_reqs = lengths.shape[0]
    model_width = out_proj.shape[1]
    q_width = queries.shape[1]

    packed = jnp.concatenate([queries, fresh_token_keys, fresh_token_values, residual_in], axis=1)
    slot_of = jnp.zeros((total_reqs,), jnp.int32).at[slot_order].set(
        jnp.arange(total_reqs, dtype=jnp.int32)
    )
    home_slots = lax.dynamic_slice_in_dim(slot_of, req_index * per_dev, per_dev)
    to_slots = (
        jnp.zeros((req_count, per_dev, packed.shape[1]), packed.dtype)
        .at[home_slots // per_dev, home_slots % per_dev]
        .set(packed)
    )
    from_homes = lax.all_to_all(to_slots, "req", 0, 0, tiled=False)
    served = lax.dynamic_slice_in_dim(slot_order, req_index * per_dev, per_dev)
    mine = from_homes[served // per_dev, jnp.arange(per_dev)]
    query_rows = mine[:, :q_width].reshape(per_dev, -1, head_dim)
    self_key_row = mine[:, q_width:q_width + head_dim]
    self_value_row = mine[:, q_width + head_dim:q_width + 2 * head_dim]
    residual_rows = mine[:, q_width + 2 * head_dim:]
    live_len = lengths[served]

    inv_root = 1.0 / math.sqrt(head_dim)
    scores = (
        jnp.einsum("rqd,rld->rql", query_rows, cached_key_slots, preferred_element_type=jnp.float32)
        * inv_root
    )
    positions = jnp.arange(cached_key_slots.shape[1])
    scores = jnp.where((positions[None, :] < live_len[:, None])[:, None, :], scores, -1e30)
    own_score = (
        jnp.einsum("rqd,rd->rq", query_rows, self_key_row, preferred_element_type=jnp.float32)
        * inv_root
    )
    highest = jnp.maximum(jnp.max(scores, axis=2), own_score)
    weights = jnp.exp(scores - highest[:, :, None])
    own_weight = jnp.exp(own_score - highest)
    totals = jnp.sum(weights, axis=2) + own_weight
    numerator = jnp.einsum(
        "rql,rld->rqd",
        weights.astype(jnp.bfloat16),
        cached_value_slots,
        preferred_element_type=jnp.float32,
    )
    own_low = lax.optimization_barrier(own_weight.astype(jnp.bfloat16)).astype(jnp.float32)
    numerator = numerator + own_low[:, :, None] * self_value_row.astype(jnp.float32)[:, None, :]
    attended = (numerator / totals[:, :, None]).astype(jnp.bfloat16).reshape(per_dev, -1)
    projected = jnp.dot(attended, out_proj, preferred_element_type=jnp.float32)

    col_start = kv_index * col_count
    own_cols = jnp.concatenate(
        [residual_rows.astype(jnp.float32), norm_gain.astype(jnp.float32)[None, :]], axis=0
    )
    summed_in = jnp.concatenate(
        [projected, jnp.zeros((1, model_width), jnp.float32)], axis=0
    ) + lax.dynamic_update_slice(
        jnp.zeros((per_dev + 1, model_width), jnp.float32), own_cols, (0, col_start)
    )
    parts = [summed_in] + [
        lax.ppermute(summed_in, "kv", [(i, (i + shift) % kv_count) for i in range(kv_count)])
        for shift in range(1, kv_count)
    ]
    stacked = jnp.stack(parts)[(kv_index - jnp.arange(kv_count)) % kv_count]
    summed = stacked[0]
    for source in range(1, kv_count):
        summed = summed + stacked[source]
    hidden = summed[:per_dev]
    gain = summed[per_dev]
    squares = jnp.sum(hidden * hidden, axis=1)
    normed = (hidden * lax.rsqrt(squares / model_width + 1e-06)[:, None] * gain).astype(
        jnp.bfloat16
    )
    local_count = gate_proj.shape[0]
    served_ids = expert_ids[served] // local_count
    wanted = jnp.any(
        served_ids[None, :, :] == jnp.arange(req_count, dtype=jnp.int32)[:, None, None], axis=2
    )
    to_experts = jnp.where(wanted[:, :, None], normed[None, :, :], jnp.zeros_like(normed)[None])
    by_slot = lax.all_to_all(to_experts, "req", 0, 0, tiled=False)

    capacity = min(2 * total_reqs * expert_ids.shape[1] // (local_count * req_count), total_reqs)
    expert = req_index * local_count + 0
    named_here = expert_ids == expert
    token_gate = jnp.sum(jnp.where(named_here, gate_values, 0.0), axis=1)
    uses_expert = jnp.any(named_here, axis=1)
    picked = jnp.nonzero(uses_expert, size=capacity, fill_value=0)[0].astype(jnp.int32)
    valid_rows = jnp.arange(capacity) < jnp.sum(uses_expert.astype(jnp.int32))
    picked_slots = slot_of[picked]
    row_block = by_slot[picked_slots // per_dev, picked_slots % per_dev]
    gate_h = jnp.dot(row_block, gate_proj[0], preferred_element_type=jnp.float32)
    up_h = jnp.dot(row_block, up_proj[0], preferred_element_type=jnp.float32)
    inner_act = (jax.nn.silu(gate_h) * up_h).astype(jnp.bfloat16)
    outputs = jnp.dot(inner_act, down_proj[0], preferred_element_type=jnp.float32)
    row_gate = jnp.where(valid_rows, token_gate[picked], 0.0)
    weighted = outputs * row_gate[:, None]
    weighted = lax.dynamic_slice_in_dim(weighted, col_start, col_count, axis=1) + sum(
        lax.ppermute(
            lax.dynamic_slice_in_dim(
                weighted, ((kv_index + shift) % kv_count) * col_count, col_count, axis=1
            ),
            "kv",
            [(i, (i + shift) % kv_count) for i in range(kv_count)],
        )
        for shift in range(1, kv_count)
    )

    own_hidden = lax.dynamic_slice_in_dim(hidden, col_start, col_count, axis=1)
    combined = (
        jnp.zeros((req_count, per_dev, col_count), jnp.float32)
        .at[picked // per_dev, picked % per_dev]
        .add(weighted)
        .at[served // per_dev, served % per_dev]
        .add(own_hidden)
    )
    layer_rows = jnp.sum(lax.all_to_all(combined, "req", 0, 0, tiled=False), axis=0)
    return layer_rows.astype(jnp.bfloat16)


def solution(mesh):
    in_specs = (
        P("req", "kv"),
        P("req", "kv"),
        P("req", "kv"),
        P("req", "kv"),
        P("req", None, "kv"),
        P("req", None, "kv"),
        P(),
        P(),
        P("kv", None),
        P("kv"),
        P(),
        P(),
        P("req", None, "kv"),
        P("req", None, "kv"),
        P("req", "kv", None),
    )
    out_specs = P("req", "kv")
    return jax.shard_map(
        per_device, mesh=mesh, in_specs=in_specs, out_specs=out_specs, check_vma=False
    )
```

```python
import math

import jax
import jax.numpy as jnp
from jax import lax
from jax.sharding import PartitionSpec as P


def per_device(
    residual_in,
    queries,
    fresh_token_keys,
    fresh_token_values,
    cached_key_slots,
    cached_value_slots,
    lengths,
    slot_order,
    out_proj,
    norm_gain,
    expert_ids,
    gate_values,
    gate_proj,
    up_proj,
    down_proj,
):
    req_count = lax.axis_size("req")
    kv_count = lax.axis_size("kv")
    req_index = lax.axis_index("req")
    kv_index = lax.axis_index("kv")
    per_dev = residual_in.shape[0]
    head_dim = fresh_token_keys.shape[1]
    col_count = residual_in.shape[1]
    total_reqs = lengths.shape[0]
    model_width = out_proj.shape[1]
    q_width = queries.shape[1]

    packed = jnp.concatenate([queries, fresh_token_keys, fresh_token_values, residual_in], axis=1)
    slot_of = jnp.zeros((total_reqs,), jnp.int32).at[slot_order].set(
        jnp.arange(total_reqs, dtype=jnp.int32)
    )
    slots_grid = slot_order.reshape(req_count, per_dev)
    to_slots = jnp.where(
        (slots_grid // per_dev == req_index)[:, :, None],
        packed[slots_grid % per_dev],
        jnp.zeros((), packed.dtype),
    )
    from_homes = lax.all_to_all(to_slots, "req", 0, 0, tiled=False)
    served = lax.dynamic_slice_in_dim(slot_order, req_index * per_dev, per_dev)
    mine = from_homes[served // per_dev, jnp.arange(per_dev)]
    query_rows = mine[:, :q_width].reshape(per_dev, -1, head_dim)
    self_key_row = mine[:, q_width:q_width + head_dim]
    self_value_row = mine[:, q_width + head_dim:q_width + 2 * head_dim]
    residual_rows = mine[:, q_width + 2 * head_dim:]
    live_len = lengths[served]

    inv_root = 1.0 / math.sqrt(head_dim)
    scores = (
        jnp.einsum("rqd,rld->rql", query_rows, cached_key_slots, preferred_element_type=jnp.float32)
        * inv_root
    )
    positions = jnp.arange(cached_key_slots.shape[1])
    scores = jnp.where((positions[None, :] < live_len[:, None])[:, None, :], scores, -1e30)
    own_score = (
        jnp.einsum("rqd,rd->rq", query_rows, self_key_row, preferred_element_type=jnp.float32)
        * inv_root
    )
    highest = jnp.maximum(jnp.max(scores, axis=2), own_score)
    weights = jnp.exp(scores - highest[:, :, None])
    own_weight = jnp.exp(own_score - highest)
    totals = jnp.sum(weights, axis=2) + own_weight
    numerator = jnp.einsum(
        "rql,rld->rqd",
        weights.astype(jnp.bfloat16),
        cached_value_slots,
        preferred_element_type=jnp.float32,
    )
    own_low = lax.optimization_barrier(own_weight.astype(jnp.bfloat16)).astype(jnp.float32)
    numerator = numerator + own_low[:, :, None] * self_value_row.astype(jnp.float32)[:, None, :]
    attended = (numerator / totals[:, :, None]).astype(jnp.bfloat16).reshape(per_dev, -1)
    projected = jnp.dot(attended, out_proj, preferred_element_type=jnp.float32)

    col_start = kv_index * col_count
    own_cols = jnp.concatenate(
        [residual_rows.astype(jnp.float32), norm_gain.astype(jnp.float32)[None, :]], axis=0
    )
    summed_in = jnp.concatenate(
        [projected, jnp.zeros((1, model_width), jnp.float32)], axis=0
    ) + lax.dynamic_update_slice(
        jnp.zeros((per_dev + 1, model_width), jnp.float32), own_cols, (0, col_start)
    )
    parts = [summed_in] + [
        lax.ppermute(summed_in, "kv", [(i, (i + shift) % kv_count) for i in range(kv_count)])
        for shift in range(1, kv_count)
    ]
    stacked = jnp.stack(parts)[(kv_index - jnp.arange(kv_count)) % kv_count]
    summed = stacked[0]
    for source in range(1, kv_count):
        summed = summed + stacked[source]
    hidden = summed[:per_dev]
    gain = summed[per_dev]
    squares = jnp.sum(hidden * hidden, axis=1)
    normed = (hidden * lax.rsqrt(squares / model_width + 1e-06)[:, None] * gain).astype(
        jnp.bfloat16
    )
    local_count = gate_proj.shape[0]
    served_ids = expert_ids[served] // local_count
    wanted = jnp.any(
        served_ids[None, :, :] == jnp.arange(req_count, dtype=jnp.int32)[:, None, None], axis=2
    )
    to_experts = jnp.where(wanted[:, :, None], normed[None, :, :], jnp.zeros_like(normed)[None])
    by_slot = lax.all_to_all(to_experts, "req", 0, 0, tiled=False)

    capacity = min(2 * total_reqs * expert_ids.shape[1] // (local_count * req_count), total_reqs)
    expert = req_index * local_count + 0
    named_here = expert_ids == expert
    token_gate = jnp.sum(jnp.where(named_here, gate_values, 0.0), axis=1)
    uses_expert = jnp.any(named_here, axis=1)
    picked = jnp.nonzero(uses_expert, size=capacity, fill_value=0)[0].astype(jnp.int32)
    valid_rows = jnp.arange(capacity) < jnp.sum(uses_expert.astype(jnp.int32))
    picked_slots = slot_of[picked]
    row_block = by_slot[picked_slots // per_dev, picked_slots % per_dev]
    gate_h = jnp.dot(row_block, gate_proj[0], preferred_element_type=jnp.float32)
    up_h = jnp.dot(row_block, up_proj[0], preferred_element_type=jnp.float32)
    inner_act = (jax.nn.silu(gate_h) * up_h).astype(jnp.bfloat16)
    outputs = jnp.dot(inner_act, down_proj[0], preferred_element_type=jnp.float32)
    row_gate = jnp.where(valid_rows, token_gate[picked], 0.0)
    weighted = outputs * row_gate[:, None]
    weighted = lax.dynamic_slice_in_dim(weighted, col_start, col_count, axis=1) + sum(
        lax.ppermute(
            lax.dynamic_slice_in_dim(
                weighted, ((kv_index + shift) % kv_count) * col_count, col_count, axis=1
            ),
            "kv",
            [(i, (i + shift) % kv_count) for i in range(kv_count)],
        )
        for shift in range(1, kv_count)
    )

    own_hidden = lax.dynamic_slice_in_dim(hidden, col_start, col_count, axis=1)
    at_pick = jnp.where(uses_expert, jnp.cumsum(uses_expert.astype(jnp.int32)) - 1, capacity)
    weighted_ext = jnp.concatenate([weighted, jnp.zeros((1, col_count), jnp.float32)], axis=0)
    slot_grid = slot_of.reshape(req_count, per_dev)
    combined = weighted_ext[at_pick.reshape(req_count, per_dev)] + jnp.where(
        (slot_grid // per_dev == req_index)[:, :, None],
        own_hidden[slot_grid % per_dev],
        0.0,
    )
    layer_rows = jnp.sum(lax.all_to_all(combined, "req", 0, 0, tiled=False), axis=0)
    return layer_rows.astype(jnp.bfloat16)


def solution(mesh):
    in_specs = (
        P("req", "kv"),
        P("req", "kv"),
        P("req", "kv"),
        P("req", "kv"),
        P("req", None, "kv"),
        P("req", None, "kv"),
        P(),
        P(),
        P("kv", None),
        P("kv"),
        P(),
        P(),
        P("req", None, "kv"),
        P("req", None, "kv"),
        P("req", "kv", None),
    )
    out_specs = P("req", "kv")
    return jax.shard_map(
        per_device, mesh=mesh, in_specs=in_specs, out_specs=out_specs, check_vma=False
    )
```

```python
import math

import jax
import jax.numpy as jnp
from jax import lax
from jax.sharding import PartitionSpec as P


def per_device(
    residual_in,
    queries,
    fresh_token_keys,
    fresh_token_values,
    cached_key_slots,
    cached_value_slots,
    lengths,
    slot_order,
    out_proj,
    norm_gain,
    expert_ids,
    gate_values,
    gate_proj,
    up_proj,
    down_proj,
):
    req_count = lax.axis_size("req")
    kv_count = lax.axis_size("kv")
    req_index = lax.axis_index("req")
    kv_index = lax.axis_index("kv")
    per_dev = residual_in.shape[0]
    head_dim = fresh_token_keys.shape[1]
    col_count = residual_in.shape[1]
    total_reqs = lengths.shape[0]
    model_width = out_proj.shape[1]
    q_width = queries.shape[1]

    packed = jnp.concatenate([queries, fresh_token_keys, fresh_token_values, residual_in], axis=1)
    slot_of = jnp.zeros((total_reqs,), jnp.int32).at[slot_order].set(
        jnp.arange(total_reqs, dtype=jnp.int32)
    )
    pack_width = packed.shape[1]

    def pick_row(rows, which):
        chosen = rows[0][None, :]
        for i in range(1, rows.shape[0]):
            chosen = jnp.where((which == i)[:, None], rows[i][None, :], chosen)
        return chosen

    to_slots = jnp.concatenate(
        [
            jnp.where(
                (slot_order[j::per_dev] // per_dev == req_index)[:, None],
                pick_row(packed, slot_order[j::per_dev] % per_dev),
                jnp.zeros((), packed.dtype),
            )
            for j in range(per_dev)
        ],
        axis=1,
    )
    from_homes = lax.all_to_all(to_slots, "req", 0, 0, tiled=True)
    served = lax.dynamic_slice_in_dim(slot_order, req_index * per_dev, per_dev)
    mine = jnp.stack(
        [
            lax.dynamic_slice(from_homes, (served[j] // per_dev, j * pack_width), (1, pack_width))[0]
            for j in range(per_dev)
        ]
    )
    query_rows = mine[:, :q_width].reshape(per_dev, -1, head_dim)
    self_key_row = mine[:, q_width:q_width + head_dim]
    self_value_row = mine[:, q_width + head_dim:q_width + 2 * head_dim]
    residual_rows = mine[:, q_width + 2 * head_dim:]
    live_len = lengths[served]

    inv_root = 1.0 / math.sqrt(head_dim)
    scores = (
        jnp.einsum("rqd,rld->rql", query_rows, cached_key_slots, preferred_element_type=jnp.float32)
        * inv_root
    )
    positions = jnp.arange(cached_key_slots.shape[1])
    scores = jnp.where((positions[None, :] < live_len[:, None])[:, None, :], scores, -1e30)
    own_score = (
        jnp.einsum("rqd,rd->rq", query_rows, self_key_row, preferred_element_type=jnp.float32)
        * inv_root
    )
    highest = jnp.maximum(jnp.max(scores, axis=2), own_score)
    weights = jnp.exp(scores - highest[:, :, None])
    own_weight = jnp.exp(own_score - highest)
    totals = jnp.sum(weights, axis=2) + own_weight
    numerator = jnp.einsum(
        "rql,rld->rqd",
        weights.astype(jnp.bfloat16),
        cached_value_slots,
        preferred_element_type=jnp.float32,
    )
    own_low = lax.optimization_barrier(own_weight.astype(jnp.bfloat16)).astype(jnp.float32)
    numerator = numerator + own_low[:, :, None] * self_value_row.astype(jnp.float32)[:, None, :]
    attended = (numerator / totals[:, :, None]).astype(jnp.bfloat16).reshape(per_dev, -1)
    projected = jnp.dot(attended, out_proj, preferred_element_type=jnp.float32)

    col_start = kv_index * col_count
    own_cols = jnp.concatenate(
        [residual_rows.astype(jnp.float32), norm_gain.astype(jnp.float32)[None, :]], axis=0
    )
    summed_in = jnp.concatenate(
        [projected, jnp.zeros((1, model_width), jnp.float32)], axis=0
    ) + lax.dynamic_update_slice(
        jnp.zeros((per_dev + 1, model_width), jnp.float32), own_cols, (0, col_start)
    )
    parts = [summed_in] + [
        lax.ppermute(summed_in, "kv", [(i, (i + shift) % kv_count) for i in range(kv_count)])
        for shift in range(1, kv_count)
    ]
    stacked = jnp.stack(parts)[(kv_index - jnp.arange(kv_count)) % kv_count]
    summed = stacked[0]
    for source in range(1, kv_count):
        summed = summed + stacked[source]
    hidden = summed[:per_dev]
    gain = summed[per_dev]
    squares = jnp.sum(hidden * hidden, axis=1)
    normed = (hidden * lax.rsqrt(squares / model_width + 1e-06)[:, None] * gain).astype(
        jnp.bfloat16
    )
    local_count = gate_proj.shape[0]
    served_ids = expert_ids[served] // local_count
    wanted = jnp.any(
        served_ids[None, :, :] == jnp.arange(req_count, dtype=jnp.int32)[:, None, None], axis=2
    )
    to_experts = jnp.concatenate(
        [
            jnp.where(wanted[:, j, None], normed[j][None, :], jnp.zeros((), normed.dtype))
            for j in range(per_dev)
        ],
        axis=1,
    )
    by_slot = lax.all_to_all(to_experts, "req", 0, 0, tiled=True)

    capacity = min(2 * total_reqs * expert_ids.shape[1] // (local_count * req_count), total_reqs)
    expert = req_index * local_count + 0
    named_here = expert_ids == expert
    token_gate = jnp.sum(jnp.where(named_here, gate_values, 0.0), axis=1)
    uses_expert = jnp.any(named_here, axis=1)
    picked = jnp.nonzero(uses_expert, size=capacity, fill_value=0)[0].astype(jnp.int32)
    valid_rows = jnp.arange(capacity) < jnp.sum(uses_expert.astype(jnp.int32))
    picked_slots = slot_of[picked]
    picked_pairs = by_slot[picked_slots // per_dev]
    row_block = picked_pairs[:, :model_width]
    for j in range(1, per_dev):
        row_block = jnp.where(
            (picked_slots % per_dev == j)[:, None],
            picked_pairs[:, j * model_width:(j + 1) * model_width],
            row_block,
        )
    gate_h = jnp.dot(row_block, gate_proj[0], preferred_element_type=jnp.float32)
    up_h = jnp.dot(row_block, up_proj[0], preferred_element_type=jnp.float32)
    inner_act = (jax.nn.silu(gate_h) * up_h).astype(jnp.bfloat16)
    outputs = jnp.dot(inner_act, down_proj[0], preferred_element_type=jnp.float32)
    row_gate = jnp.where(valid_rows, token_gate[picked], 0.0)
    weighted = outputs * row_gate[:, None]
    weighted = lax.dynamic_slice_in_dim(weighted, col_start, col_count, axis=1) + sum(
        lax.ppermute(
            lax.dynamic_slice_in_dim(
                weighted, ((kv_index + shift) % kv_count) * col_count, col_count, axis=1
            ),
            "kv",
            [(i, (i + shift) % kv_count) for i in range(kv_count)],
        )
        for shift in range(1, kv_count)
    )

    own_hidden = lax.dynamic_slice_in_dim(hidden, col_start, col_count, axis=1)
    at_pick = jnp.where(uses_expert, jnp.cumsum(uses_expert.astype(jnp.int32)) - 1, capacity)
    weighted_ext = jnp.concatenate([weighted, jnp.zeros((1, col_count), jnp.float32)], axis=0)
    halves = []
    for j in range(per_dev):
        home_slot = slot_of[j::per_dev]
        halves.append(
            weighted_ext[at_pick[j::per_dev]]
            + jnp.where(
                (home_slot // per_dev == req_index)[:, None],
                pick_row(own_hidden, home_slot % per_dev),
                0.0,
            )
        )
    combined = jnp.concatenate(halves, axis=1)
    totals_out = jnp.sum(lax.all_to_all(combined, "req", 0, 0, tiled=True), axis=0)
    layer_rows = totals_out.reshape(per_dev, col_count)
    return layer_rows.astype(jnp.bfloat16)


def solution(mesh):
    in_specs = (
        P("req", "kv"),
        P("req", "kv"),
        P("req", "kv"),
        P("req", "kv"),
        P("req", None, "kv"),
        P("req", None, "kv"),
        P(),
        P(),
        P("kv", None),
        P("kv"),
        P(),
        P(),
        P("req", None, "kv"),
        P("req", None, "kv"),
        P("req", "kv", None),
    )
    out_specs = P("req", "kv")
    return jax.shard_map(
        per_device, mesh=mesh, in_specs=in_specs, out_specs=out_specs, check_vma=False
    )
```

```python
import math

import jax
import jax.numpy as jnp
from jax import lax
from jax.sharding import PartitionSpec as P


def per_device(
    residual_in,
    queries,
    fresh_token_keys,
    fresh_token_values,
    cached_key_slots,
    cached_value_slots,
    lengths,
    slot_order,
    out_proj,
    norm_gain,
    expert_ids,
    gate_values,
    gate_proj,
    up_proj,
    down_proj,
):
    req_count = lax.axis_size("req")
    kv_count = lax.axis_size("kv")
    req_index = lax.axis_index("req")
    kv_index = lax.axis_index("kv")
    per_dev = residual_in.shape[0]
    head_dim = fresh_token_keys.shape[1]
    col_count = residual_in.shape[1]
    total_reqs = lengths.shape[0]
    model_width = out_proj.shape[1]
    q_width = queries.shape[1]

    packed = jnp.concatenate([queries, fresh_token_keys, fresh_token_values, residual_in], axis=1)
    slot_of = jnp.zeros((total_reqs,), jnp.int32).at[slot_order].set(
        jnp.arange(total_reqs, dtype=jnp.int32)
    )
    slots_grid = slot_order.reshape(req_count, per_dev)
    from_grid = slots_grid % per_dev
    to_slots = jnp.broadcast_to(packed[0], (req_count, per_dev, packed.shape[1]))
    for i in range(1, per_dev):
        to_slots = jnp.where((from_grid == i)[:, :, None], packed[i][None, None, :], to_slots)
    to_slots = jnp.where(
        (slots_grid // per_dev == req_index)[:, :, None], to_slots, jnp.zeros((), packed.dtype)
    )
    from_homes = lax.all_to_all(to_slots, "req", 0, 0, tiled=False)
    served = lax.dynamic_slice_in_dim(slot_order, req_index * per_dev, per_dev)
    mine = from_homes[served // per_dev, jnp.arange(per_dev)]
    query_rows = mine[:, :q_width].reshape(per_dev, -1, head_dim)
    self_key_row = mine[:, q_width:q_width + head_dim]
    self_value_row = mine[:, q_width + head_dim:q_width + 2 * head_dim]
    residual_rows = mine[:, q_width + 2 * head_dim:]
    live_len = lengths[served]

    inv_root = 1.0 / math.sqrt(head_dim)
    scores = (
        jnp.einsum("rqd,rld->rql", query_rows, cached_key_slots, preferred_element_type=jnp.float32)
        * inv_root
    )
    positions = jnp.arange(cached_key_slots.shape[1])
    scores = jnp.where((positions[None, :] < live_len[:, None])[:, None, :], scores, -1e30)
    own_score = (
        jnp.einsum("rqd,rd->rq", query_rows, self_key_row, preferred_element_type=jnp.float32)
        * inv_root
    )
    highest = jnp.maximum(jnp.max(scores, axis=2), own_score)
    weights = jnp.exp(scores - highest[:, :, None])
    own_weight = jnp.exp(own_score - highest)
    totals = jnp.sum(weights, axis=2) + own_weight
    numerator = jnp.einsum(
        "rql,rld->rqd",
        weights.astype(jnp.bfloat16),
        cached_value_slots,
        preferred_element_type=jnp.float32,
    )
    own_low = lax.optimization_barrier(own_weight.astype(jnp.bfloat16)).astype(jnp.float32)
    numerator = numerator + own_low[:, :, None] * self_value_row.astype(jnp.float32)[:, None, :]
    attended = (numerator / totals[:, :, None]).astype(jnp.bfloat16).reshape(per_dev, -1)
    projected = jnp.dot(attended, out_proj, preferred_element_type=jnp.float32)

    col_start = kv_index * col_count
    own_cols = jnp.concatenate(
        [residual_rows.astype(jnp.float32), norm_gain.astype(jnp.float32)[None, :]], axis=0
    )
    summed_in = jnp.concatenate(
        [projected, jnp.zeros((1, model_width), jnp.float32)], axis=0
    ) + lax.dynamic_update_slice(
        jnp.zeros((per_dev + 1, model_width), jnp.float32), own_cols, (0, col_start)
    )
    parts = [summed_in] + [
        lax.ppermute(summed_in, "kv", [(i, (i + shift) % kv_count) for i in range(kv_count)])
        for shift in range(1, kv_count)
    ]
    stacked = jnp.stack(parts)[(kv_index - jnp.arange(kv_count)) % kv_count]
    summed = stacked[0]
    for source in range(1, kv_count):
        summed = summed + stacked[source]
    hidden = summed[:per_dev]
    gain = summed[per_dev]
    squares = jnp.sum(hidden * hidden, axis=1)
    normed = (hidden * lax.rsqrt(squares / model_width + 1e-06)[:, None] * gain).astype(
        jnp.bfloat16
    )
    local_count = gate_proj.shape[0]
    served_ids = expert_ids[served] // local_count
    wanted = jnp.any(
        served_ids[None, :, :] == jnp.arange(req_count, dtype=jnp.int32)[:, None, None], axis=2
    )
    to_experts = jnp.where(wanted[:, :, None], normed[None, :, :], jnp.zeros_like(normed)[None])
    by_slot = lax.all_to_all(to_experts, "req", 0, 0, tiled=False)

    capacity = min(2 * total_reqs * expert_ids.shape[1] // (local_count * req_count), total_reqs)
    expert = req_index * local_count + 0
    named_here = expert_ids == expert
    token_gate = jnp.sum(jnp.where(named_here, gate_values, 0.0), axis=1)
    uses_expert = jnp.any(named_here, axis=1)
    picked = jnp.nonzero(uses_expert, size=capacity, fill_value=0)[0].astype(jnp.int32)
    valid_rows = jnp.arange(capacity) < jnp.sum(uses_expert.astype(jnp.int32))
    picked_slots = slot_of[picked]
    row_block = by_slot[picked_slots // per_dev, picked_slots % per_dev]
    gate_h = jnp.dot(row_block, gate_proj[0], preferred_element_type=jnp.float32)
    up_h = jnp.dot(row_block, up_proj[0], preferred_element_type=jnp.float32)
    inner_act = (jax.nn.silu(gate_h) * up_h).astype(jnp.bfloat16)
    outputs = jnp.dot(inner_act, down_proj[0], preferred_element_type=jnp.float32)
    row_gate = jnp.where(valid_rows, token_gate[picked], 0.0)
    weighted = outputs * row_gate[:, None]
    weighted = lax.dynamic_slice_in_dim(weighted, col_start, col_count, axis=1) + sum(
        lax.ppermute(
            lax.dynamic_slice_in_dim(
                weighted, ((kv_index + shift) % kv_count) * col_count, col_count, axis=1
            ),
            "kv",
            [(i, (i + shift) % kv_count) for i in range(kv_count)],
        )
        for shift in range(1, kv_count)
    )

    own_hidden = lax.dynamic_slice_in_dim(hidden, col_start, col_count, axis=1)
    at_pick = jnp.where(uses_expert, jnp.cumsum(uses_expert.astype(jnp.int32)) - 1, capacity)
    weighted_ext = jnp.concatenate([weighted, jnp.zeros((1, col_count), jnp.float32)], axis=0)
    halves = []
    for j in range(per_dev):
        home_slot = slot_of[j::per_dev]
        own_row = own_hidden[0][None, :]
        for i in range(1, per_dev):
            own_row = jnp.where((home_slot % per_dev == i)[:, None], own_hidden[i][None, :], own_row)
        halves.append(
            weighted_ext[at_pick[j::per_dev]]
            + jnp.where((home_slot // per_dev == req_index)[:, None], own_row, 0.0)
        )
    combined = jnp.concatenate(halves, axis=1)
    totals_out = jnp.sum(lax.all_to_all(combined, "req", 0, 0, tiled=True), axis=0)
    layer_rows = totals_out.reshape(per_dev, col_count)
    return layer_rows.astype(jnp.bfloat16)


def solution(mesh):
    in_specs = (
        P("req", "kv"),
        P("req", "kv"),
        P("req", "kv"),
        P("req", "kv"),
        P("req", None, "kv"),
        P("req", None, "kv"),
        P(),
        P(),
        P("kv", None),
        P("kv"),
        P(),
        P(),
        P("req", None, "kv"),
        P("req", None, "kv"),
        P("req", "kv", None),
    )
    out_specs = P("req", "kv")
    return jax.shard_map(
        per_device, mesh=mesh, in_specs=in_specs, out_specs=out_specs, check_vma=False
    )
```

```python
import math

import jax
import jax.numpy as jnp
from jax import lax
from jax.sharding import PartitionSpec as P


def per_device(
    residual_in,
    queries,
    fresh_token_keys,
    fresh_token_values,
    cached_key_slots,
    cached_value_slots,
    lengths,
    slot_order,
    out_proj,
    norm_gain,
    expert_ids,
    gate_values,
    gate_proj,
    up_proj,
    down_proj,
):
    req_count = lax.axis_size("req")
    kv_count = lax.axis_size("kv")
    req_index = lax.axis_index("req")
    kv_index = lax.axis_index("kv")
    per_dev = residual_in.shape[0]
    head_dim = fresh_token_keys.shape[1]
    col_count = residual_in.shape[1]
    total_reqs = lengths.shape[0]
    model_width = out_proj.shape[1]
    q_width = queries.shape[1]

    pieces = (queries, fresh_token_keys, fresh_token_values, residual_in)
    slot_of = jnp.zeros((total_reqs,), jnp.int32).at[slot_order].set(
        jnp.arange(total_reqs, dtype=jnp.int32)
    )
    slots_grid = slot_order.reshape(req_count, per_dev)
    from_grid = slots_grid % per_dev
    sent_here = (slots_grid // per_dev == req_index)[:, :, None]

    def to_slot_rows(piece):
        rows = jnp.broadcast_to(piece[0], (req_count, per_dev, piece.shape[1]))
        for i in range(1, per_dev):
            rows = jnp.where((from_grid == i)[:, :, None], piece[i][None, None, :], rows)
        return jnp.where(sent_here, rows, jnp.zeros((), piece.dtype))

    to_slots = jnp.concatenate([to_slot_rows(piece) for piece in pieces], axis=2)
    from_homes = lax.all_to_all(to_slots, "req", 0, 0, tiled=False)
    served = lax.dynamic_slice_in_dim(slot_order, req_index * per_dev, per_dev)
    mine = from_homes[served // per_dev, jnp.arange(per_dev)]
    query_rows = mine[:, :q_width].reshape(per_dev, -1, head_dim)
    self_key_row = mine[:, q_width:q_width + head_dim]
    self_value_row = mine[:, q_width + head_dim:q_width + 2 * head_dim]
    residual_rows = mine[:, q_width + 2 * head_dim:]
    live_len = lengths[served]

    inv_root = 1.0 / math.sqrt(head_dim)
    scores = (
        jnp.einsum("rqd,rld->rql", query_rows, cached_key_slots, preferred_element_type=jnp.float32)
        * inv_root
    )
    positions = jnp.arange(cached_key_slots.shape[1])
    scores = jnp.where((positions[None, :] < live_len[:, None])[:, None, :], scores, -1e30)
    own_score = (
        jnp.einsum("rqd,rd->rq", query_rows, self_key_row, preferred_element_type=jnp.float32)
        * inv_root
    )
    highest = jnp.maximum(jnp.max(scores, axis=2), own_score)
    weights = jnp.exp(scores - highest[:, :, None])
    own_weight = jnp.exp(own_score - highest)
    totals = jnp.sum(weights, axis=2) + own_weight
    numerator = jnp.einsum(
        "rql,rld->rqd",
        weights.astype(jnp.bfloat16),
        cached_value_slots,
        preferred_element_type=jnp.float32,
    )
    own_low = lax.optimization_barrier(own_weight.astype(jnp.bfloat16)).astype(jnp.float32)
    numerator = numerator + own_low[:, :, None] * self_value_row.astype(jnp.float32)[:, None, :]
    attended = (numerator / totals[:, :, None]).astype(jnp.bfloat16).reshape(per_dev, -1)
    projected = jnp.dot(attended, out_proj, preferred_element_type=jnp.float32)

    col_start = kv_index * col_count
    own_cols = jnp.concatenate(
        [residual_rows.astype(jnp.float32), norm_gain.astype(jnp.float32)[None, :]], axis=0
    )
    summed_in = jnp.concatenate(
        [projected, jnp.zeros((1, model_width), jnp.float32)], axis=0
    ) + lax.dynamic_update_slice(
        jnp.zeros((per_dev + 1, model_width), jnp.float32), own_cols, (0, col_start)
    )
    parts = [summed_in] + [
        lax.ppermute(summed_in, "kv", [(i, (i + shift) % kv_count) for i in range(kv_count)])
        for shift in range(1, kv_count)
    ]
    summed = parts[0]
    for part in parts[1:]:
        summed = summed + part
    hidden = summed[:per_dev]
    gain = summed[per_dev]
    squares = jnp.sum(hidden * hidden, axis=1)
    normed = (hidden * lax.rsqrt(squares / model_width + 1e-06)[:, None] * gain).astype(
        jnp.bfloat16
    )
    local_count = gate_proj.shape[0]
    served_ids = expert_ids[served] // local_count
    wanted = jnp.any(
        served_ids[None, :, :] == jnp.arange(req_count, dtype=jnp.int32)[:, None, None], axis=2
    )
    to_experts = jnp.where(wanted[:, :, None], normed[None, :, :], jnp.zeros_like(normed)[None])
    by_slot = lax.all_to_all(to_experts, "req", 0, 0, tiled=False)

    capacity = min(2 * total_reqs * expert_ids.shape[1] // (local_count * req_count), total_reqs)
    expert = req_index * local_count + 0
    named_here = expert_ids == expert
    token_gate = jnp.sum(jnp.where(named_here, gate_values, 0.0), axis=1)
    uses_expert = jnp.any(named_here, axis=1)
    picked = jnp.nonzero(uses_expert, size=capacity, fill_value=0)[0].astype(jnp.int32)
    valid_rows = jnp.arange(capacity) < jnp.sum(uses_expert.astype(jnp.int32))
    picked_slots = slot_of[picked]
    row_block = by_slot[picked_slots // per_dev, picked_slots % per_dev]
    gate_h = jnp.dot(row_block, gate_proj[0], preferred_element_type=jnp.float32)
    up_h = jnp.dot(row_block, up_proj[0], preferred_element_type=jnp.float32)
    inner_act = (jax.nn.silu(gate_h) * up_h).astype(jnp.bfloat16)
    outputs = jnp.dot(inner_act, down_proj[0], preferred_element_type=jnp.float32)
    row_gate = jnp.where(valid_rows, token_gate[picked], 0.0)
    weighted = outputs * row_gate[:, None]
    weighted = lax.dynamic_slice_in_dim(weighted, col_start, col_count, axis=1) + sum(
        lax.ppermute(
            lax.dynamic_slice_in_dim(
                weighted, ((kv_index + shift) % kv_count) * col_count, col_count, axis=1
            ),
            "kv",
            [(i, (i + shift) % kv_count) for i in range(kv_count)],
        )
        for shift in range(1, kv_count)
    )

    own_hidden = lax.dynamic_slice_in_dim(hidden, col_start, col_count, axis=1)
    at_pick = jnp.where(uses_expert, jnp.cumsum(uses_expert.astype(jnp.int32)) - 1, capacity)
    weighted_ext = jnp.concatenate([weighted, jnp.zeros((1, col_count), jnp.float32)], axis=0)
    halves = []
    for j in range(per_dev):
        home_slot = slot_of[j::per_dev]
        own_row = own_hidden[0][None, :]
        for i in range(1, per_dev):
            own_row = jnp.where((home_slot % per_dev == i)[:, None], own_hidden[i][None, :], own_row)
        halves.append(
            weighted_ext[at_pick[j::per_dev]]
            + jnp.where((home_slot // per_dev == req_index)[:, None], own_row, 0.0)
        )
    combined = jnp.concatenate(halves, axis=1)
    totals_out = jnp.sum(lax.all_to_all(combined, "req", 0, 0, tiled=True), axis=0)
    layer_rows = totals_out.reshape(per_dev, col_count)
    return layer_rows.astype(jnp.bfloat16)


def solution(mesh):
    in_specs = (
        P("req", "kv"),
        P("req", "kv"),
        P("req", "kv"),
        P("req", "kv"),
        P("req", None, "kv"),
        P("req", None, "kv"),
        P(),
        P(),
        P("kv", None),
        P("kv"),
        P(),
        P(),
        P("req", None, "kv"),
        P("req", None, "kv"),
        P("req", "kv", None),
    )
    out_specs = P("req", "kv")
    return jax.shard_map(
        per_device, mesh=mesh, in_specs=in_specs, out_specs=out_specs, check_vma=False
    )
```

```python
import math

import jax
import jax.numpy as jnp
from jax import lax
from jax.experimental import pallas as pl
from jax.experimental.pallas import tpu as pltpu
from jax.sharding import PartitionSpec as P


def _ffn_body(x_ref, wg_ref, wu_ref, wd_ref, gate_ref, out_ref):
    step = pl.program_id(0)

    @pl.when(step == 0)
    def _():
        out_ref[...] = jnp.zeros_like(out_ref)

    x = x_ref[...]
    gate_h = jnp.dot(x, wg_ref[...], preferred_element_type=jnp.float32)
    up_h = jnp.dot(x, wu_ref[...], preferred_element_type=jnp.float32)
    inner = (gate_h / (1.0 + jnp.exp(-gate_h)) * up_h).astype(jnp.bfloat16)
    out_ref[...] += jnp.dot(inner, wd_ref[...], preferred_element_type=jnp.float32)

    @pl.when(step == pl.num_programs(0) - 1)
    def _():
        out_ref[...] = out_ref[...] * gate_ref[...]

def expert_ffn(x, wg, wu, wd, row_gate, block=128):
    rows, width = x.shape
    hidden = wg.shape[1]
    return pl.pallas_call(
        _ffn_body,
        grid=(hidden // block,),
        in_specs=[
            pl.BlockSpec((rows, width), lambda h: (0, 0)),
            pl.BlockSpec((width, block), lambda h: (0, h)),
            pl.BlockSpec((width, block), lambda h: (0, h)),
            pl.BlockSpec((block, width), lambda h: (h, 0)),
            pl.BlockSpec((rows, 1), lambda h: (0, 0)),
        ],
        out_specs=pl.BlockSpec((rows, width), lambda h: (0, 0)),
        out_shape=jax.ShapeDtypeStruct((rows, width), jnp.float32),
        compiler_params=pltpu.CompilerParams(dimension_semantics=("arbitrary",)),
    )(x, wg, wu, wd, row_gate)


def per_device(
    residual_in,
    queries,
    fresh_token_keys,
    fresh_token_values,
    cached_key_slots,
    cached_value_slots,
    lengths,
    slot_order,
    out_proj,
    norm_gain,
    expert_ids,
    gate_values,
    gate_proj,
    up_proj,
    down_proj,
):
    req_count = lax.axis_size("req")
    kv_count = lax.axis_size("kv")
    req_index = lax.axis_index("req")
    kv_index = lax.axis_index("kv")
    per_dev = residual_in.shape[0]
    head_dim = fresh_token_keys.shape[1]
    col_count = residual_in.shape[1]
    total_reqs = lengths.shape[0]
    model_width = out_proj.shape[1]
    q_width = queries.shape[1]

    pieces = (queries, fresh_token_keys, fresh_token_values, residual_in)
    slot_of = jnp.zeros((total_reqs,), jnp.int32).at[slot_order].set(
        jnp.arange(total_reqs, dtype=jnp.int32)
    )
    slots_grid = slot_order.reshape(req_count, per_dev)
    from_grid = slots_grid % per_dev
    sent_here = (slots_grid // per_dev == req_index)[:, :, None]

    def to_slot_rows(piece):
        rows = jnp.broadcast_to(piece[0], (req_count, per_dev, piece.shape[1]))
        for i in range(1, per_dev):
            rows = jnp.where((from_grid == i)[:, :, None], piece[i][None, None, :], rows)
        return jnp.where(sent_here, rows, jnp.zeros((), piece.dtype))

    to_slots = jnp.concatenate([to_slot_rows(piece) for piece in pieces], axis=2)
    from_homes = lax.all_to_all(to_slots, "req", 0, 0, tiled=False)
    served = lax.dynamic_slice_in_dim(slot_order, req_index * per_dev, per_dev)
    mine = from_homes[served // per_dev, jnp.arange(per_dev)]
    query_rows = mine[:, :q_width].reshape(per_dev, -1, head_dim)
    self_key_row = mine[:, q_width:q_width + head_dim]
    self_value_row = mine[:, q_width + head_dim:q_width + 2 * head_dim]
    residual_rows = mine[:, q_width + 2 * head_dim:]
    live_len = lengths[served]

    inv_root = 1.0 / math.sqrt(head_dim)
    scores = (
        jnp.einsum("rqd,rld->rql", query_rows, cached_key_slots, preferred_element_type=jnp.float32)
        * inv_root
    )
    positions = jnp.arange(cached_key_slots.shape[1])
    scores = jnp.where((positions[None, :] < live_len[:, None])[:, None, :], scores, -1e30)
    own_score = (
        jnp.einsum("rqd,rd->rq", query_rows, self_key_row, preferred_element_type=jnp.float32)
        * inv_root
    )
    highest = jnp.maximum(jnp.max(scores, axis=2), own_score)
    weights = jnp.exp(scores - highest[:, :, None])
    own_weight = jnp.exp(own_score - highest)
    totals = jnp.sum(weights, axis=2) + own_weight
    numerator = jnp.einsum(
        "rql,rld->rqd",
        weights.astype(jnp.bfloat16),
        cached_value_slots,
        preferred_element_type=jnp.float32,
    )
    own_low = lax.optimization_barrier(own_weight.astype(jnp.bfloat16)).astype(jnp.float32)
    numerator = numerator + own_low[:, :, None] * self_value_row.astype(jnp.float32)[:, None, :]
    attended = (numerator / totals[:, :, None]).astype(jnp.bfloat16).reshape(per_dev, -1)
    projected = jnp.dot(attended, out_proj, preferred_element_type=jnp.float32)

    col_start = kv_index * col_count
    own_cols = jnp.concatenate(
        [residual_rows.astype(jnp.float32), norm_gain.astype(jnp.float32)[None, :]], axis=0
    )
    summed_in = jnp.concatenate(
        [projected, jnp.zeros((1, model_width), jnp.float32)], axis=0
    ) + lax.dynamic_update_slice(
        jnp.zeros((per_dev + 1, model_width), jnp.float32), own_cols, (0, col_start)
    )
    parts = [summed_in] + [
        lax.ppermute(summed_in, "kv", [(i, (i + shift) % kv_count) for i in range(kv_count)])
        for shift in range(1, kv_count)
    ]
    summed = parts[0]
    for part in parts[1:]:
        summed = summed + part
    hidden = summed[:per_dev]
    gain = summed[per_dev]
    squares = jnp.sum(hidden * hidden, axis=1)
    normed = (hidden * lax.rsqrt(squares / model_width + 1e-06)[:, None] * gain).astype(
        jnp.bfloat16
    )
    local_count = gate_proj.shape[0]
    served_ids = expert_ids[served] // local_count
    wanted = jnp.any(
        served_ids[None, :, :] == jnp.arange(req_count, dtype=jnp.int32)[:, None, None], axis=2
    )
    to_experts = jnp.where(wanted[:, :, None], normed[None, :, :], jnp.zeros_like(normed)[None])
    by_slot = lax.all_to_all(to_experts, "req", 0, 0, tiled=False)

    capacity = min(2 * total_reqs * expert_ids.shape[1] // (local_count * req_count), total_reqs)
    expert = req_index * local_count + 0
    named_here = expert_ids == expert
    token_gate = jnp.sum(jnp.where(named_here, gate_values, 0.0), axis=1)
    uses_expert = jnp.any(named_here, axis=1)
    picked = jnp.nonzero(uses_expert, size=capacity, fill_value=0)[0].astype(jnp.int32)
    valid_rows = jnp.arange(capacity) < jnp.sum(uses_expert.astype(jnp.int32))
    picked_slots = slot_of[picked]
    row_block = by_slot[picked_slots // per_dev, picked_slots % per_dev]
    row_gate = jnp.where(valid_rows, token_gate[picked], 0.0)
    weighted = expert_ffn(row_block, gate_proj[0], up_proj[0], down_proj[0], row_gate[:, None])

    weighted = lax.dynamic_slice_in_dim(weighted, col_start, col_count, axis=1) + sum(
        lax.ppermute(
            lax.dynamic_slice_in_dim(
                weighted, ((kv_index + shift) % kv_count) * col_count, col_count, axis=1
            ),
            "kv",
            [(i, (i + shift) % kv_count) for i in range(kv_count)],
        )
        for shift in range(1, kv_count)
    )

    own_hidden = lax.dynamic_slice_in_dim(hidden, col_start, col_count, axis=1)
    at_pick = jnp.where(uses_expert, jnp.cumsum(uses_expert.astype(jnp.int32)) - 1, capacity)
    weighted_ext = jnp.concatenate([weighted, jnp.zeros((1, col_count), jnp.float32)], axis=0)
    halves = []
    for j in range(per_dev):
        home_slot = slot_of[j::per_dev]
        own_row = own_hidden[0][None, :]
        for i in range(1, per_dev):
            own_row = jnp.where((home_slot % per_dev == i)[:, None], own_hidden[i][None, :], own_row)
        halves.append(
            weighted_ext[at_pick[j::per_dev]]
            + jnp.where((home_slot // per_dev == req_index)[:, None], own_row, 0.0)
        )
    combined = jnp.concatenate(halves, axis=1)
    totals_out = jnp.sum(lax.all_to_all(combined, "req", 0, 0, tiled=True), axis=0)
    layer_rows = totals_out.reshape(per_dev, col_count)
    return layer_rows.astype(jnp.bfloat16)


def solution(mesh):
    in_specs = (
        P("req", "kv"),
        P("req", "kv"),
        P("req", "kv"),
        P("req", "kv"),
        P("req", None, "kv"),
        P("req", None, "kv"),
        P(),
        P(),
        P("kv", None),
        P("kv"),
        P(),
        P(),
        P("req", None, "kv"),
        P("req", None, "kv"),
        P("req", "kv", None),
    )
    out_specs = P("req", "kv")
    return jax.shard_map(
        per_device, mesh=mesh, in_specs=in_specs, out_specs=out_specs, check_vma=False
    )
```

```python
import math

import jax
import jax.numpy as jnp
from jax import lax
from jax.sharding import PartitionSpec as P


def per_device(
    residual_in,
    queries,
    fresh_token_keys,
    fresh_token_values,
    cached_key_slots,
    cached_value_slots,
    lengths,
    slot_order,
    out_proj,
    norm_gain,
    expert_ids,
    gate_values,
    gate_proj,
    up_proj,
    down_proj,
):
    req_count = lax.axis_size("req")
    kv_count = lax.axis_size("kv")
    req_index = lax.axis_index("req")
    kv_index = lax.axis_index("kv")
    per_dev = residual_in.shape[0]
    head_dim = fresh_token_keys.shape[1]
    col_count = residual_in.shape[1]
    total_reqs = lengths.shape[0]
    model_width = out_proj.shape[1]
    q_width = queries.shape[1]

    pieces = (queries, fresh_token_keys, fresh_token_values, residual_in)
    slot_of = jnp.zeros((total_reqs,), jnp.int32).at[slot_order].set(
        jnp.arange(total_reqs, dtype=jnp.int32)
    )
    slots_grid = slot_order.reshape(req_count, per_dev)
    from_grid = slots_grid % per_dev
    sent_here = (slots_grid // per_dev == req_index)[:, :, None]

    def to_slot_rows(piece):
        rows = jnp.broadcast_to(piece[0], (req_count, per_dev, piece.shape[1]))
        for i in range(1, per_dev):
            rows = jnp.where((from_grid == i)[:, :, None], piece[i][None, None, :], rows)
        return jnp.where(sent_here, rows, jnp.zeros((), piece.dtype))

    to_slots = jnp.concatenate([to_slot_rows(piece) for piece in pieces], axis=2)
    from_homes = lax.all_to_all(to_slots, "req", 0, 0, tiled=False)
    served = lax.dynamic_slice_in_dim(slot_order, req_index * per_dev, per_dev)
    mine = from_homes[served // per_dev, jnp.arange(per_dev)]
    query_rows = mine[:, :q_width].reshape(per_dev, -1, head_dim)
    self_key_row = mine[:, q_width:q_width + head_dim]
    self_value_row = mine[:, q_width + head_dim:q_width + 2 * head_dim]
    residual_rows = mine[:, q_width + 2 * head_dim:]
    live_len = lengths[served]

    inv_root = 1.0 / math.sqrt(head_dim)
    scores = (
        jnp.einsum("rqd,rld->rql", query_rows, cached_key_slots, preferred_element_type=jnp.float32)
        * inv_root
    )
    positions = jnp.arange(cached_key_slots.shape[1])
    scores = jnp.where((positions[None, :] < live_len[:, None])[:, None, :], scores, -1e30)
    own_score = (
        jnp.einsum("rqd,rd->rq", query_rows, self_key_row, preferred_element_type=jnp.float32)
        * inv_root
    )
    highest = jnp.maximum(jnp.max(scores, axis=2), own_score)
    weights = jnp.exp(scores - highest[:, :, None])
    own_weight = jnp.exp(own_score - highest)
    totals = jnp.sum(weights, axis=2) + own_weight
    numerator = jnp.einsum(
        "rql,rld->rqd",
        weights.astype(jnp.bfloat16),
        cached_value_slots,
        preferred_element_type=jnp.float32,
    )
    own_low = lax.optimization_barrier(own_weight.astype(jnp.bfloat16)).astype(jnp.float32)
    numerator = numerator + own_low[:, :, None] * self_value_row.astype(jnp.float32)[:, None, :]
    attended = (numerator / totals[:, :, None]).astype(jnp.bfloat16).reshape(per_dev, -1)
    projected = jnp.dot(attended, out_proj, preferred_element_type=jnp.float32)

    col_start = kv_index * col_count
    summed_in = projected + lax.dynamic_update_slice(
        jnp.zeros((per_dev, model_width), jnp.float32),
        residual_rows.astype(jnp.float32),
        (0, col_start),
    )
    parts = [summed_in] + [
        lax.ppermute(summed_in, "kv", [(i, (i + shift) % kv_count) for i in range(kv_count)])
        for shift in range(1, kv_count)
    ]
    summed = parts[0]
    for part in parts[1:]:
        summed = summed + part
    hidden = summed
    squares = jnp.sum(hidden * hidden, axis=1)
    own_hidden = lax.dynamic_slice_in_dim(hidden, col_start, col_count, axis=1)
    normed = (
        own_hidden
        * lax.rsqrt(squares / model_width + 1e-06)[:, None]
        * norm_gain.astype(jnp.float32)[None, :]
    ).astype(jnp.bfloat16)
    local_count = gate_proj.shape[0]
    served_ids = expert_ids[served] // local_count
    wanted = jnp.any(
        served_ids[None, :, :] == jnp.arange(req_count, dtype=jnp.int32)[:, None, None], axis=2
    )
    to_experts = jnp.where(wanted[:, :, None], normed[None, :, :], jnp.zeros_like(normed)[None])
    by_slot = lax.all_to_all(to_experts, "req", 0, 0, tiled=False)

    capacity = min(2 * total_reqs * expert_ids.shape[1] // (local_count * req_count), total_reqs)
    expert = req_index * local_count + 0
    named_here = expert_ids == expert
    token_gate = jnp.sum(jnp.where(named_here, gate_values, 0.0), axis=1)
    uses_expert = jnp.any(named_here, axis=1)
    picked = jnp.nonzero(uses_expert, size=capacity, fill_value=0)[0].astype(jnp.int32)
    valid_rows = jnp.arange(capacity) < jnp.sum(uses_expert.astype(jnp.int32))
    picked_slots = slot_of[picked]
    row_block = by_slot[picked_slots // per_dev, picked_slots % per_dev]
    kv_shifts = range(1, kv_count)
    from_peers = [
        lax.ppermute(row_block, "kv", [(i, (i + shift) % kv_count) for i in range(kv_count)])
        for shift in kv_shifts
    ]

    def block_rows(weights, source):
        return lax.dynamic_slice_in_dim(weights, source * col_count, col_count, axis=0)

    gate_h = jnp.dot(row_block, block_rows(gate_proj[0], kv_index), preferred_element_type=jnp.float32)
    up_h = jnp.dot(row_block, block_rows(up_proj[0], kv_index), preferred_element_type=jnp.float32)
    for shift, peer_rows in zip(kv_shifts, from_peers):
        source = (kv_index - shift) % kv_count
        gate_h = gate_h + jnp.dot(
            peer_rows, block_rows(gate_proj[0], source), preferred_element_type=jnp.float32
        )
        up_h = up_h + jnp.dot(
            peer_rows, block_rows(up_proj[0], source), preferred_element_type=jnp.float32
        )
    inner_act = (jax.nn.silu(gate_h) * up_h).astype(jnp.bfloat16)
    outputs = jnp.dot(inner_act, down_proj[0], preferred_element_type=jnp.float32)
    row_gate = jnp.where(valid_rows, token_gate[picked], 0.0)
    weighted = outputs * row_gate[:, None]
    weighted = lax.dynamic_slice_in_dim(weighted, col_start, col_count, axis=1) + sum(
        lax.ppermute(
            lax.dynamic_slice_in_dim(
                weighted, ((kv_index + shift) % kv_count) * col_count, col_count, axis=1
            ),
            "kv",
            [(i, (i + shift) % kv_count) for i in range(kv_count)],
        )
        for shift in range(1, kv_count)
    )

    at_pick = jnp.where(uses_expert, jnp.cumsum(uses_expert.astype(jnp.int32)) - 1, capacity)
    weighted_ext = jnp.concatenate([weighted, jnp.zeros((1, col_count), jnp.float32)], axis=0)
    halves = []
    for j in range(per_dev):
        home_slot = slot_of[j::per_dev]
        own_row = own_hidden[0][None, :]
        for i in range(1, per_dev):
            own_row = jnp.where((home_slot % per_dev == i)[:, None], own_hidden[i][None, :], own_row)
        halves.append(
            weighted_ext[at_pick[j::per_dev]]
            + jnp.where((home_slot // per_dev == req_index)[:, None], own_row, 0.0)
        )
    combined = jnp.concatenate(halves, axis=1)
    totals_out = jnp.sum(lax.all_to_all(combined, "req", 0, 0, tiled=True), axis=0)
    layer_rows = totals_out.reshape(per_dev, col_count)
    return layer_rows.astype(jnp.bfloat16)


def solution(mesh):
    in_specs = (
        P("req", "kv"),
        P("req", "kv"),
        P("req", "kv"),
        P("req", "kv"),
        P("req", None, "kv"),
        P("req", None, "kv"),
        P(),
        P(),
        P("kv", None),
        P("kv"),
        P(),
        P(),
        P("req", None, "kv"),
        P("req", None, "kv"),
        P("req", "kv", None),
    )
    out_specs = P("req", "kv")
    return jax.shard_map(
        per_device, mesh=mesh, in_specs=in_specs, out_specs=out_specs, check_vma=False
    )
```

```python
import math

import jax
import jax.numpy as jnp
from jax import lax
from jax.sharding import PartitionSpec as P


def per_device(
    residual_in,
    queries,
    fresh_token_keys,
    fresh_token_values,
    cached_key_slots,
    cached_value_slots,
    lengths,
    slot_order,
    out_proj,
    norm_gain,
    expert_ids,
    gate_values,
    gate_proj,
    up_proj,
    down_proj,
):
    req_count = lax.axis_size("req")
    kv_count = lax.axis_size("kv")
    req_index = lax.axis_index("req")
    kv_index = lax.axis_index("kv")
    per_dev = residual_in.shape[0]
    head_dim = fresh_token_keys.shape[1]
    col_count = residual_in.shape[1]
    total_reqs = lengths.shape[0]
    model_width = out_proj.shape[1]
    q_width = queries.shape[1]

    pieces = (queries, fresh_token_keys, fresh_token_values, residual_in)
    slot_of = jnp.zeros((total_reqs,), jnp.int32).at[slot_order].set(
        jnp.arange(total_reqs, dtype=jnp.int32)
    )
    slots_grid = slot_order.reshape(req_count, per_dev)
    from_grid = slots_grid % per_dev
    sent_here = (slots_grid // per_dev == req_index)[:, :, None]

    def to_slot_rows(piece):
        rows = jnp.broadcast_to(piece[0], (req_count, per_dev, piece.shape[1]))
        for i in range(1, per_dev):
            rows = jnp.where((from_grid == i)[:, :, None], piece[i][None, None, :], rows)
        return jnp.where(sent_here, rows, jnp.zeros((), piece.dtype))

    to_slots = jnp.concatenate([to_slot_rows(piece) for piece in pieces], axis=2)
    from_homes = lax.all_to_all(to_slots, "req", 0, 0, tiled=False)
    served = lax.dynamic_slice_in_dim(slot_order, req_index * per_dev, per_dev)
    mine = from_homes[served // per_dev, jnp.arange(per_dev)]
    query_rows = mine[:, :q_width].reshape(per_dev, -1, head_dim)
    self_key_row = mine[:, q_width:q_width + head_dim]
    self_value_row = mine[:, q_width + head_dim:q_width + 2 * head_dim]
    residual_rows = mine[:, q_width + 2 * head_dim:]
    live_len = lengths[served]

    inv_root = 1.0 / math.sqrt(head_dim)
    scores = (
        jnp.einsum("rqd,rld->rql", query_rows, cached_key_slots, preferred_element_type=jnp.float32)
        * inv_root
    )
    positions = jnp.arange(cached_key_slots.shape[1])
    scores = jnp.where((positions[None, :] < live_len[:, None])[:, None, :], scores, -1e30)
    own_score = (
        jnp.einsum("rqd,rd->rq", query_rows, self_key_row, preferred_element_type=jnp.float32)
        * inv_root
    )
    highest = jnp.maximum(jnp.max(scores, axis=2), own_score)
    weights = jnp.exp(scores - highest[:, :, None])
    own_weight = jnp.exp(own_score - highest)
    totals = jnp.sum(weights, axis=2) + own_weight
    numerator = jnp.einsum(
        "rql,rld->rqd",
        weights.astype(jnp.bfloat16),
        cached_value_slots,
        preferred_element_type=jnp.float32,
    )
    own_low = lax.optimization_barrier(own_weight.astype(jnp.bfloat16)).astype(jnp.float32)
    numerator = numerator + own_low[:, :, None] * self_value_row.astype(jnp.float32)[:, None, :]
    attended = (numerator / totals[:, :, None]).astype(jnp.bfloat16).reshape(per_dev, -1)
    projected = jnp.dot(attended, out_proj, preferred_element_type=jnp.float32)

    col_start = kv_index * col_count
    summed_in = projected + lax.dynamic_update_slice(
        jnp.zeros((per_dev, model_width), jnp.float32),
        residual_rows.astype(jnp.float32),
        (0, col_start),
    )
    parts = [summed_in] + [
        lax.ppermute(summed_in, "kv", [(i, (i + shift) % kv_count) for i in range(kv_count)])
        for shift in range(1, kv_count)
    ]
    summed = parts[0]
    for part in parts[1:]:
        summed = summed + part
    hidden = summed
    squares = jnp.sum(hidden * hidden, axis=1)
    own_hidden = lax.dynamic_slice_in_dim(hidden, col_start, col_count, axis=1)
    normed = (
        own_hidden
        * lax.rsqrt(squares / model_width + 1e-06)[:, None]
        * norm_gain.astype(jnp.float32)[None, :]
    ).astype(jnp.bfloat16)
    local_count = gate_proj.shape[0]
    served_ids = expert_ids[served] // local_count
    wanted = jnp.any(
        served_ids[None, :, :] == jnp.arange(req_count, dtype=jnp.int32)[:, None, None], axis=2
    )
    to_experts = jnp.where(wanted[:, :, None], normed[None, :, :], jnp.zeros_like(normed)[None])
    by_slot = lax.all_to_all(to_experts, "req", 0, 0, tiled=False)

    capacity = min(2 * total_reqs * expert_ids.shape[1] // (local_count * req_count), total_reqs)
    expert = req_index * local_count + 0
    named_here = expert_ids == expert
    token_gate = jnp.sum(jnp.where(named_here, gate_values, 0.0), axis=1)
    uses_expert = jnp.any(named_here, axis=1)
    picked = jnp.nonzero(uses_expert, size=capacity, fill_value=0)[0].astype(jnp.int32)
    valid_rows = jnp.arange(capacity) < jnp.sum(uses_expert.astype(jnp.int32))
    picked_slots = slot_of[picked]
    row_block = by_slot[picked_slots // per_dev, picked_slots % per_dev]
    kv_shifts = range(1, kv_count)
    from_peers = [
        lax.ppermute(row_block, "kv", [(i, (i + shift) % kv_count) for i in range(kv_count)])
        for shift in kv_shifts
    ]

    def block_rows(weights, source):
        return lax.dynamic_slice_in_dim(weights, source * col_count, col_count, axis=0)

    gate_h = jnp.dot(row_block, block_rows(gate_proj[0], kv_index), preferred_element_type=jnp.float32)
    up_h = jnp.dot(row_block, block_rows(up_proj[0], kv_index), preferred_element_type=jnp.float32)
    for shift, peer_rows in zip(kv_shifts, from_peers):
        source = (kv_index - shift) % kv_count
        gate_h = gate_h + jnp.dot(
            peer_rows, block_rows(gate_proj[0], source), preferred_element_type=jnp.float32
        )
        up_h = up_h + jnp.dot(
            peer_rows, block_rows(up_proj[0], source), preferred_element_type=jnp.float32
        )
    inner_act = (jax.nn.silu(gate_h) * up_h).astype(jnp.bfloat16)
    outputs = jnp.dot(inner_act, down_proj[0], preferred_element_type=jnp.float32)
    row_gate = jnp.where(valid_rows, token_gate[picked], 0.0)
    weighted = outputs * row_gate[:, None]
    weighted = lax.dynamic_slice_in_dim(weighted, col_start, col_count, axis=1) + sum(
        lax.ppermute(
            lax.dynamic_slice_in_dim(
                weighted, ((kv_index + shift) % kv_count) * col_count, col_count, axis=1
            ),
            "kv",
            [(i, (i + shift) % kv_count) for i in range(kv_count)],
        )
        for shift in range(1, kv_count)
    )

    at_pick = jnp.where(uses_expert, jnp.cumsum(uses_expert.astype(jnp.int32)) - 1, capacity)
    weighted_ext = jnp.concatenate([weighted, jnp.zeros((1, col_count), jnp.float32)], axis=0)
    halves = []
    for j in range(per_dev):
        home_slot = slot_of[j::per_dev]
        own_row = own_hidden[0][None, :]
        for i in range(1, per_dev):
            own_row = jnp.where((home_slot % per_dev == i)[:, None], own_hidden[i][None, :], own_row)
        halves.append(
            weighted_ext[at_pick[j::per_dev]]
            + jnp.where((home_slot // per_dev == req_index)[:, None], own_row, 0.0)
        )
    combined = jnp.stack(halves, axis=1).astype(jnp.bfloat16)
    layer_rows = jnp.sum(
        lax.all_to_all(combined, "req", 0, 0, tiled=False).astype(jnp.float32), axis=0
    )
    return layer_rows.astype(jnp.bfloat16)


def solution(mesh):
    in_specs = (
        P("req", "kv"),
        P("req", "kv"),
        P("req", "kv"),
        P("req", "kv"),
        P("req", None, "kv"),
        P("req", None, "kv"),
        P(),
        P(),
        P("kv", None),
        P("kv"),
        P(),
        P(),
        P("req", None, "kv"),
        P("req", None, "kv"),
        P("req", "kv", None),
    )
    out_specs = P("req", "kv")
    return jax.shard_map(
        per_device, mesh=mesh, in_specs=in_specs, out_specs=out_specs, check_vma=False
    )
```

```python
import math

import jax
import jax.numpy as jnp
from jax import lax
from jax.experimental import pallas as pl
from jax.experimental.pallas import tpu as pltpu
from jax.sharding import PartitionSpec as P


def _ffn_body(x_ref, wg_ref, wu_ref, wd_ref, gate_ref, out_ref):
    step = pl.program_id(0)

    @pl.when(step == 0)
    def _():
        out_ref[...] = jnp.zeros_like(out_ref)

    x = x_ref[...]
    gate_h = jnp.dot(x, wg_ref[...], preferred_element_type=jnp.float32)
    up_h = jnp.dot(x, wu_ref[...], preferred_element_type=jnp.float32)
    inner = (gate_h / (1.0 + jnp.exp(-gate_h)) * up_h).astype(jnp.bfloat16)
    out_ref[...] += jnp.dot(inner, wd_ref[...], preferred_element_type=jnp.float32)

    @pl.when(step == pl.num_programs(0) - 1)
    def _():
        out_ref[...] = out_ref[...] * gate_ref[...]

def expert_ffn(x, wg, wu, wd, row_gate, block=128):
    rows, width = x.shape
    hidden = wg.shape[1]
    return pl.pallas_call(
        _ffn_body,
        grid=(hidden // block,),
        in_specs=[
            pl.BlockSpec((rows, width), lambda h: (0, 0)),
            pl.BlockSpec((width, block), lambda h: (0, h)),
            pl.BlockSpec((width, block), lambda h: (0, h)),
            pl.BlockSpec((block, width), lambda h: (h, 0)),
            pl.BlockSpec((rows, 1), lambda h: (0, 0)),
        ],
        out_specs=pl.BlockSpec((rows, width), lambda h: (0, 0)),
        out_shape=jax.ShapeDtypeStruct((rows, width), jnp.float32),
        compiler_params=pltpu.CompilerParams(dimension_semantics=("arbitrary",)),
    )(x, wg, wu, wd, row_gate)


def per_device(
    residual_in,
    queries,
    fresh_token_keys,
    fresh_token_values,
    cached_key_slots,
    cached_value_slots,
    lengths,
    slot_order,
    out_proj,
    norm_gain,
    expert_ids,
    gate_values,
    gate_proj,
    up_proj,
    down_proj,
):
    req_count = lax.axis_size("req")
    kv_count = lax.axis_size("kv")
    req_index = lax.axis_index("req")
    kv_index = lax.axis_index("kv")
    per_dev = residual_in.shape[0]
    head_dim = fresh_token_keys.shape[1]
    col_count = residual_in.shape[1]
    total_reqs = lengths.shape[0]
    model_width = out_proj.shape[1]
    q_width = queries.shape[1]

    pieces = (queries, fresh_token_keys, fresh_token_values, residual_in)
    slot_of = jnp.zeros((total_reqs,), jnp.int32).at[slot_order].set(
        jnp.arange(total_reqs, dtype=jnp.int32)
    )
    slots_grid = slot_order.reshape(req_count, per_dev)
    from_grid = slots_grid % per_dev
    sent_here = (slots_grid // per_dev == req_index)[:, :, None]

    def to_slot_rows(piece):
        rows = jnp.broadcast_to(piece[0], (req_count, per_dev, piece.shape[1]))
        for i in range(1, per_dev):
            rows = jnp.where((from_grid == i)[:, :, None], piece[i][None, None, :], rows)
        return jnp.where(sent_here, rows, jnp.zeros((), piece.dtype))

    to_slots = jnp.concatenate([to_slot_rows(piece) for piece in pieces], axis=2)
    from_homes = lax.all_to_all(to_slots, "req", 0, 0, tiled=False)
    served = lax.dynamic_slice_in_dim(slot_order, req_index * per_dev, per_dev)
    mine = from_homes[served // per_dev, jnp.arange(per_dev)]
    query_rows = mine[:, :q_width].reshape(per_dev, -1, head_dim)
    self_key_row = mine[:, q_width:q_width + head_dim]
    self_value_row = mine[:, q_width + head_dim:q_width + 2 * head_dim]
    residual_rows = mine[:, q_width + 2 * head_dim:]
    live_len = lengths[served]

    inv_root = 1.0 / math.sqrt(head_dim)
    scores = (
        jnp.einsum("rqd,rld->rql", query_rows, cached_key_slots, preferred_element_type=jnp.float32)
        * inv_root
    )
    positions = jnp.arange(cached_key_slots.shape[1])
    scores = jnp.where((positions[None, :] < live_len[:, None])[:, None, :], scores, -1e30)
    own_score = (
        jnp.einsum("rqd,rd->rq", query_rows, self_key_row, preferred_element_type=jnp.float32)
        * inv_root
    )
    highest = jnp.maximum(jnp.max(scores, axis=2), own_score)
    weights = jnp.exp(scores - highest[:, :, None])
    own_weight = jnp.exp(own_score - highest)
    totals = jnp.sum(weights, axis=2) + own_weight
    numerator = jnp.einsum(
        "rql,rld->rqd",
        weights.astype(jnp.bfloat16),
        cached_value_slots,
        preferred_element_type=jnp.float32,
    )
    own_low = lax.optimization_barrier(own_weight.astype(jnp.bfloat16)).astype(jnp.float32)
    numerator = numerator + own_low[:, :, None] * self_value_row.astype(jnp.float32)[:, None, :]
    attended = (numerator / totals[:, :, None]).astype(jnp.bfloat16).reshape(per_dev, -1)
    projected = jnp.dot(attended, out_proj, preferred_element_type=jnp.float32)

    col_start = kv_index * col_count
    summed_in = projected + lax.dynamic_update_slice(
        jnp.zeros((per_dev, model_width), jnp.float32),
        residual_rows.astype(jnp.float32),
        (0, col_start),
    )
    parts = [summed_in] + [
        lax.ppermute(summed_in, "kv", [(i, (i + shift) % kv_count) for i in range(kv_count)])
        for shift in range(1, kv_count)
    ]
    summed = parts[0]
    for part in parts[1:]:
        summed = summed + part
    hidden = summed
    squares = jnp.sum(hidden * hidden, axis=1)
    own_hidden = lax.dynamic_slice_in_dim(hidden, col_start, col_count, axis=1)
    normed = (
        own_hidden
        * lax.rsqrt(squares / model_width + 1e-06)[:, None]
        * norm_gain.astype(jnp.float32)[None, :]
    ).astype(jnp.bfloat16)
    local_count = gate_proj.shape[0]
    served_ids = expert_ids[served] // local_count
    wanted = jnp.any(
        served_ids[None, :, :] == jnp.arange(req_count, dtype=jnp.int32)[:, None, None], axis=2
    )
    to_experts = jnp.where(wanted[:, :, None], normed[None, :, :], jnp.zeros_like(normed)[None])
    by_slot = lax.all_to_all(to_experts, "req", 0, 0, tiled=False)

    capacity = min(2 * total_reqs * expert_ids.shape[1] // (local_count * req_count), total_reqs)
    expert = req_index * local_count + 0
    named_here = expert_ids == expert
    token_gate = jnp.sum(jnp.where(named_here, gate_values, 0.0), axis=1)
    uses_expert = jnp.any(named_here, axis=1)
    picked = jnp.nonzero(uses_expert, size=capacity, fill_value=0)[0].astype(jnp.int32)
    valid_rows = jnp.arange(capacity) < jnp.sum(uses_expert.astype(jnp.int32))
    picked_slots = slot_of[picked]
    row_block = by_slot[picked_slots // per_dev, picked_slots % per_dev]
    kv_shifts = range(1, kv_count)
    from_peers = [
        lax.ppermute(row_block, "kv", [(i, (i + shift) % kv_count) for i in range(kv_count)])
        for shift in kv_shifts
    ]

    candidates = [row_block] + from_peers
    in_order = []
    for block in range(kv_count):
        chosen = candidates[0]
        for shift in kv_shifts:
            chosen = jnp.where((kv_index - shift) % kv_count == block, candidates[shift], chosen)
        in_order.append(chosen)
    full_rows = jnp.concatenate(in_order, axis=1)
    row_gate = jnp.where(valid_rows, token_gate[picked], 0.0)
    weighted = expert_ffn(full_rows, gate_proj[0], up_proj[0], down_proj[0], row_gate[:, None])

    weighted = lax.dynamic_slice_in_dim(weighted, col_start, col_count, axis=1) + sum(
        lax.ppermute(
            lax.dynamic_slice_in_dim(
                weighted, ((kv_index + shift) % kv_count) * col_count, col_count, axis=1
            ),
            "kv",
            [(i, (i + shift) % kv_count) for i in range(kv_count)],
        )
        for shift in range(1, kv_count)
    )

    at_pick = jnp.where(uses_expert, jnp.cumsum(uses_expert.astype(jnp.int32)) - 1, capacity)
    weighted_ext = jnp.concatenate([weighted, jnp.zeros((1, col_count), jnp.float32)], axis=0)
    halves = []
    for j in range(per_dev):
        home_slot = slot_of[j::per_dev]
        own_row = own_hidden[0][None, :]
        for i in range(1, per_dev):
            own_row = jnp.where((home_slot % per_dev == i)[:, None], own_hidden[i][None, :], own_row)
        halves.append(
            weighted_ext[at_pick[j::per_dev]]
            + jnp.where((home_slot // per_dev == req_index)[:, None], own_row, 0.0)
        )
    combined = jnp.stack(halves, axis=1).astype(jnp.bfloat16)
    layer_rows = jnp.sum(
        lax.all_to_all(combined, "req", 0, 0, tiled=False).astype(jnp.float32), axis=0
    )
    return layer_rows.astype(jnp.bfloat16)


def solution(mesh):
    in_specs = (
        P("req", "kv"),
        P("req", "kv"),
        P("req", "kv"),
        P("req", "kv"),
        P("req", None, "kv"),
        P("req", None, "kv"),
        P(),
        P(),
        P("kv", None),
        P("kv"),
        P(),
        P(),
        P("req", None, "kv"),
        P("req", None, "kv"),
        P("req", "kv", None),
    )
    out_specs = P("req", "kv")
    return jax.shard_map(
        per_device, mesh=mesh, in_specs=in_specs, out_specs=out_specs, check_vma=False
    )
```

```python
import math

import jax
import jax.numpy as jnp
from jax import lax
from jax.sharding import PartitionSpec as P


def per_device(
    residual_in,
    queries,
    fresh_token_keys,
    fresh_token_values,
    cached_key_slots,
    cached_value_slots,
    lengths,
    slot_order,
    out_proj,
    norm_gain,
    expert_ids,
    gate_values,
    gate_proj,
    up_proj,
    down_proj,
):
    req_count = lax.axis_size("req")
    kv_count = lax.axis_size("kv")
    req_index = lax.axis_index("req")
    kv_index = lax.axis_index("kv")
    per_dev = residual_in.shape[0]
    head_dim = fresh_token_keys.shape[1]
    col_count = residual_in.shape[1]
    total_reqs = lengths.shape[0]
    model_width = out_proj.shape[1]
    q_width = queries.shape[1]

    pieces = (queries, fresh_token_keys, fresh_token_values, residual_in)
    slot_of = jnp.zeros((total_reqs,), jnp.int32).at[slot_order].set(
        jnp.arange(total_reqs, dtype=jnp.int32)
    )
    slots_grid = slot_order.reshape(req_count, per_dev)
    from_grid = slots_grid % per_dev
    sent_here = (slots_grid // per_dev == req_index)[:, :, None]

    def to_slot_rows(piece):
        rows = jnp.broadcast_to(piece[0], (req_count, per_dev, piece.shape[1]))
        for i in range(1, per_dev):
            rows = jnp.where((from_grid == i)[:, :, None], piece[i][None, None, :], rows)
        return jnp.where(sent_here, rows, jnp.zeros((), piece.dtype))

    to_slots = jnp.concatenate([to_slot_rows(piece) for piece in pieces], axis=2)
    from_homes = lax.all_to_all(to_slots, "req", 0, 0, tiled=False)
    served = lax.dynamic_slice_in_dim(slot_order, req_index * per_dev, per_dev)
    mine = from_homes[served // per_dev, jnp.arange(per_dev)]
    query_rows = mine[:, :q_width].reshape(per_dev, -1, head_dim)
    self_key_row = mine[:, q_width:q_width + head_dim]
    self_value_row = mine[:, q_width + head_dim:q_width + 2 * head_dim]
    residual_rows = mine[:, q_width + 2 * head_dim:]
    live_len = lengths[served]

    inv_root = 1.0 / math.sqrt(head_dim)
    scores = (
        jnp.einsum("rqd,rld->rql", query_rows, cached_key_slots, preferred_element_type=jnp.float32)
        * inv_root
    )
    positions = jnp.arange(cached_key_slots.shape[1])
    scores = jnp.where((positions[None, :] < live_len[:, None])[:, None, :], scores, -1e30)
    own_score = (
        jnp.einsum("rqd,rd->rq", query_rows, self_key_row, preferred_element_type=jnp.float32)
        * inv_root
    )
    highest = jnp.maximum(jnp.max(scores, axis=2), own_score)
    weights = jnp.exp(scores - highest[:, :, None])
    own_weight = jnp.exp(own_score - highest)
    totals = jnp.sum(weights, axis=2) + own_weight
    numerator = jnp.einsum(
        "rql,rld->rqd",
        weights.astype(jnp.bfloat16),
        cached_value_slots,
        preferred_element_type=jnp.float32,
    )
    own_low = lax.optimization_barrier(own_weight.astype(jnp.bfloat16)).astype(jnp.float32)
    numerator = numerator + own_low[:, :, None] * self_value_row.astype(jnp.float32)[:, None, :]
    attended = (numerator / totals[:, :, None]).astype(jnp.bfloat16).reshape(per_dev, -1)
    projected = jnp.dot(attended, out_proj, preferred_element_type=jnp.float32)

    col_start = kv_index * col_count
    summed_in = projected + lax.dynamic_update_slice(
        jnp.zeros((per_dev, model_width), jnp.float32),
        residual_rows.astype(jnp.float32),
        (0, col_start),
    )
    parts = [summed_in] + [
        lax.ppermute(summed_in, "kv", [(i, (i + shift) % kv_count) for i in range(kv_count)])
        for shift in range(1, kv_count)
    ]
    summed = parts[0]
    for part in parts[1:]:
        summed = summed + part
    hidden = summed
    squares = jnp.sum(hidden * hidden, axis=1)
    own_hidden = lax.dynamic_slice_in_dim(hidden, col_start, col_count, axis=1)
    normed = (
        own_hidden
        * lax.rsqrt(squares / model_width + 1e-06)[:, None]
        * norm_gain.astype(jnp.float32)[None, :]
    ).astype(jnp.bfloat16)
    hidden_part = []
    for j in range(per_dev):
        home_slot = slot_of[j::per_dev]
        own_row = own_hidden[0][None, :]
        for i in range(1, per_dev):
            own_row = jnp.where((home_slot % per_dev == i)[:, None], own_hidden[i][None, :], own_row)
        hidden_part.append(jnp.where((home_slot // per_dev == req_index)[:, None], own_row, 0.0))
    local_count = gate_proj.shape[0]
    served_ids = expert_ids[served] // local_count
    wanted = jnp.any(
        served_ids[None, :, :] == jnp.arange(req_count, dtype=jnp.int32)[:, None, None], axis=2
    )
    to_experts = jnp.where(wanted[:, :, None], normed[None, :, :], jnp.zeros_like(normed)[None])
    by_slot = lax.all_to_all(to_experts, "req", 0, 0, tiled=False)

    capacity = min(2 * total_reqs * expert_ids.shape[1] // (local_count * req_count), total_reqs)
    expert = req_index * local_count + 0
    named_here = expert_ids == expert
    token_gate = jnp.sum(jnp.where(named_here, gate_values, 0.0), axis=1)
    uses_expert = jnp.any(named_here, axis=1)
    picked = jnp.nonzero(uses_expert, size=capacity, fill_value=0)[0].astype(jnp.int32)
    valid_rows = jnp.arange(capacity) < jnp.sum(uses_expert.astype(jnp.int32))
    picked_slots = slot_of[picked]
    row_block = by_slot[picked_slots // per_dev, picked_slots % per_dev]
    kv_shifts = range(1, kv_count)
    from_peers = [
        lax.ppermute(row_block, "kv", [(i, (i + shift) % kv_count) for i in range(kv_count)])
        for shift in kv_shifts
    ]

    def block_rows(weights, source):
        return lax.dynamic_slice_in_dim(weights, source * col_count, col_count, axis=0)

    gate_h = jnp.dot(row_block, block_rows(gate_proj[0], kv_index), preferred_element_type=jnp.float32)
    up_h = jnp.dot(row_block, block_rows(up_proj[0], kv_index), preferred_element_type=jnp.float32)
    for shift, peer_rows in zip(kv_shifts, from_peers):
        source = (kv_index - shift) % kv_count
        gate_h = gate_h + jnp.dot(
            peer_rows, block_rows(gate_proj[0], source), preferred_element_type=jnp.float32
        )
        up_h = up_h + jnp.dot(
            peer_rows, block_rows(up_proj[0], source), preferred_element_type=jnp.float32
        )
    inner_act = (jax.nn.silu(gate_h) * up_h).astype(jnp.bfloat16)
    outputs = jnp.dot(inner_act, down_proj[0], preferred_element_type=jnp.float32)
    row_gate = jnp.where(valid_rows, token_gate[picked], 0.0)
    weighted = outputs * row_gate[:, None]
    weighted = lax.dynamic_slice_in_dim(weighted, col_start, col_count, axis=1) + sum(
        lax.ppermute(
            lax.dynamic_slice_in_dim(
                weighted, ((kv_index + shift) % kv_count) * col_count, col_count, axis=1
            ),
            "kv",
            [(i, (i + shift) % kv_count) for i in range(kv_count)],
        )
        for shift in range(1, kv_count)
    )

    at_pick = jnp.where(uses_expert, jnp.cumsum(uses_expert.astype(jnp.int32)) - 1, capacity)
    weighted_ext = jnp.concatenate([weighted, jnp.zeros((1, col_count), jnp.float32)], axis=0)
    halves = [
        weighted_ext[at_pick[j::per_dev]] + hidden_part[j] for j in range(per_dev)
    ]
    combined = jnp.stack(halves, axis=1).astype(jnp.bfloat16)
    layer_rows = jnp.sum(
        lax.all_to_all(combined, "req", 0, 0, tiled=False).astype(jnp.float32), axis=0
    )
    return layer_rows.astype(jnp.bfloat16)


def solution(mesh):
    in_specs = (
        P("req", "kv"),
        P("req", "kv"),
        P("req", "kv"),
        P("req", "kv"),
        P("req", None, "kv"),
        P("req", None, "kv"),
        P(),
        P(),
        P("kv", None),
        P("kv"),
        P(),
        P(),
        P("req", None, "kv"),
        P("req", None, "kv"),
        P("req", "kv", None),
    )
    out_specs = P("req", "kv")
    return jax.shard_map(
        per_device, mesh=mesh, in_specs=in_specs, out_specs=out_specs, check_vma=False
    )
```

```python
import math

import jax
import jax.numpy as jnp
from jax import lax
from jax.sharding import PartitionSpec as P


def per_device(
    residual_in,
    queries,
    fresh_token_keys,
    fresh_token_values,
    cached_key_slots,
    cached_value_slots,
    lengths,
    slot_order,
    out_proj,
    norm_gain,
    expert_ids,
    gate_values,
    gate_proj,
    up_proj,
    down_proj,
):
    req_count = lax.axis_size("req")
    kv_count = lax.axis_size("kv")
    req_index = lax.axis_index("req")
    kv_index = lax.axis_index("kv")
    per_dev = residual_in.shape[0]
    head_dim = fresh_token_keys.shape[1]
    col_count = residual_in.shape[1]
    total_reqs = lengths.shape[0]
    model_width = out_proj.shape[1]
    q_width = queries.shape[1]

    pieces = (queries, fresh_token_keys, fresh_token_values, residual_in)
    slot_of = jnp.zeros((total_reqs,), jnp.int32).at[slot_order].set(
        jnp.arange(total_reqs, dtype=jnp.int32)
    )
    slots_grid = slot_order.reshape(req_count, per_dev)
    from_grid = slots_grid % per_dev
    sent_here = (slots_grid // per_dev == req_index)[:, :, None]

    def to_slot_rows(piece):
        rows = jnp.broadcast_to(piece[0], (req_count, per_dev, piece.shape[1]))
        for i in range(1, per_dev):
            rows = jnp.where((from_grid == i)[:, :, None], piece[i][None, None, :], rows)
        return jnp.where(sent_here, rows, jnp.zeros((), piece.dtype))

    to_slots = jnp.concatenate([to_slot_rows(piece) for piece in pieces], axis=2)
    from_homes = lax.all_to_all(to_slots, "req", 0, 0, tiled=False)
    served = lax.dynamic_slice_in_dim(slot_order, req_index * per_dev, per_dev)
    mine = from_homes[served // per_dev, jnp.arange(per_dev)]
    query_rows = mine[:, :q_width].reshape(per_dev, -1, head_dim)
    self_key_row = mine[:, q_width:q_width + head_dim]
    self_value_row = mine[:, q_width + head_dim:q_width + 2 * head_dim]
    residual_rows = mine[:, q_width + 2 * head_dim:]
    live_len = lengths[served]

    inv_root = 1.0 / math.sqrt(head_dim)
    scores = (
        jnp.einsum("rqd,rld->rql", query_rows, cached_key_slots, preferred_element_type=jnp.float32)
        * inv_root
    )
    positions = jnp.arange(cached_key_slots.shape[1])
    scores = jnp.where((positions[None, :] < live_len[:, None])[:, None, :], scores, -1e30)
    own_score = (
        jnp.einsum("rqd,rd->rq", query_rows, self_key_row, preferred_element_type=jnp.float32)
        * inv_root
    )
    highest = jnp.maximum(jnp.max(scores, axis=2), own_score)
    weights = jnp.exp(scores - highest[:, :, None])
    own_weight = jnp.exp(own_score - highest)
    totals = jnp.sum(weights, axis=2) + own_weight
    numerator = jnp.einsum(
        "rql,rld->rqd",
        weights.astype(jnp.bfloat16),
        cached_value_slots,
        preferred_element_type=jnp.float32,
    )
    own_low = lax.optimization_barrier(own_weight.astype(jnp.bfloat16)).astype(jnp.float32)
    numerator = numerator + own_low[:, :, None] * self_value_row.astype(jnp.float32)[:, None, :]
    attended = (numerator / totals[:, :, None]).astype(jnp.bfloat16).reshape(per_dev, -1)
    projected = jnp.dot(attended, out_proj, preferred_element_type=jnp.float32)

    col_start = kv_index * col_count
    summed_in = projected + lax.dynamic_update_slice(
        jnp.zeros((per_dev, model_width), jnp.float32),
        residual_rows.astype(jnp.float32),
        (0, col_start),
    )
    parts = [summed_in] + [
        lax.ppermute(summed_in, "kv", [(i, (i + shift) % kv_count) for i in range(kv_count)])
        for shift in range(1, kv_count)
    ]
    summed = parts[0]
    for part in parts[1:]:
        summed = summed + part
    hidden = summed
    squares = jnp.sum(hidden * hidden, axis=1)
    own_hidden = lax.dynamic_slice_in_dim(hidden, col_start, col_count, axis=1)
    normed = (
        own_hidden
        * lax.rsqrt(squares / model_width + 1e-06)[:, None]
        * norm_gain.astype(jnp.float32)[None, :]
    ).astype(jnp.bfloat16)
    local_count = gate_proj.shape[0]
    served_ids = expert_ids[served] // local_count
    wanted = jnp.any(
        served_ids[None, :, :] == jnp.arange(req_count, dtype=jnp.int32)[:, None, None], axis=2
    )
    to_experts = jnp.where(wanted[:, :, None], normed[None, :, :], jnp.zeros_like(normed)[None])
    by_slot = lax.all_to_all(to_experts, "req", 0, 0, tiled=False)

    capacity = min(2 * total_reqs * expert_ids.shape[1] // (local_count * req_count), total_reqs)
    expert = req_index * local_count + 0
    named_here = expert_ids == expert
    token_gate = jnp.sum(jnp.where(named_here, gate_values, 0.0), axis=1)
    uses_expert = jnp.any(named_here, axis=1)
    picked = jnp.nonzero(uses_expert, size=capacity, fill_value=0)[0].astype(jnp.int32)
    valid_rows = jnp.arange(capacity) < jnp.sum(uses_expert.astype(jnp.int32))
    picked_slots = slot_of[picked]
    row_block = by_slot[picked_slots // per_dev, picked_slots % per_dev]
    kv_shifts = range(1, kv_count)
    from_peers = [
        lax.ppermute(row_block, "kv", [(i, (i + shift) % kv_count) for i in range(kv_count)])
        for shift in kv_shifts
    ]

    def block_rows(weights, source):
        return lax.dynamic_slice_in_dim(weights, source * col_count, col_count, axis=0)

    gate_h = jnp.dot(row_block, block_rows(gate_proj[0], kv_index), preferred_element_type=jnp.float32)
    up_h = jnp.dot(row_block, block_rows(up_proj[0], kv_index), preferred_element_type=jnp.float32)
    for shift, peer_rows in zip(kv_shifts, from_peers):
        source = (kv_index - shift) % kv_count
        gate_h = gate_h + jnp.dot(
            peer_rows, block_rows(gate_proj[0], source), preferred_element_type=jnp.float32
        )
        up_h = up_h + jnp.dot(
            peer_rows, block_rows(up_proj[0], source), preferred_element_type=jnp.float32
        )
    inner_act = (jax.nn.silu(gate_h) * up_h).astype(jnp.bfloat16)
    row_gate = jnp.where(valid_rows, token_gate[picked], 0.0)

    def down_block(block):
        cols = lax.dynamic_slice_in_dim(down_proj[0], block * col_count, col_count, axis=1)
        return jnp.dot(inner_act, cols, preferred_element_type=jnp.float32) * row_gate[:, None]

    sent = [
        lax.ppermute(
            down_block((kv_index + shift) % kv_count),
            "kv",
            [(i, (i + shift) % kv_count) for i in range(kv_count)],
        )
        for shift in range(1, kv_count)
    ]
    weighted = down_block(kv_index) + sum(sent)

    at_pick = jnp.where(uses_expert, jnp.cumsum(uses_expert.astype(jnp.int32)) - 1, capacity)
    weighted_ext = jnp.concatenate([weighted, jnp.zeros((1, col_count), jnp.float32)], axis=0)
    halves = []
    for j in range(per_dev):
        home_slot = slot_of[j::per_dev]
        own_row = own_hidden[0][None, :]
        for i in range(1, per_dev):
            own_row = jnp.where((home_slot % per_dev == i)[:, None], own_hidden[i][None, :], own_row)
        halves.append(
            weighted_ext[at_pick[j::per_dev]]
            + jnp.where((home_slot // per_dev == req_index)[:, None], own_row, 0.0)
        )
    combined = jnp.stack(halves, axis=1).astype(jnp.bfloat16)
    layer_rows = jnp.sum(
        lax.all_to_all(combined, "req", 0, 0, tiled=False).astype(jnp.float32), axis=0
    )
    return layer_rows.astype(jnp.bfloat16)


def solution(mesh):
    in_specs = (
        P("req", "kv"),
        P("req", "kv"),
        P("req", "kv"),
        P("req", "kv"),
        P("req", None, "kv"),
        P("req", None, "kv"),
        P(),
        P(),
        P("kv", None),
        P("kv"),
        P(),
        P(),
        P("req", None, "kv"),
        P("req", None, "kv"),
        P("req", "kv", None),
    )
    out_specs = P("req", "kv")
    return jax.shard_map(
        per_device, mesh=mesh, in_specs=in_specs, out_specs=out_specs, check_vma=False
    )
```

```python
import math

import jax
import jax.numpy as jnp
from jax import lax
from jax.sharding import PartitionSpec as P


def per_device(
    residual_in,
    queries,
    fresh_token_keys,
    fresh_token_values,
    cached_key_slots,
    cached_value_slots,
    lengths,
    slot_order,
    out_proj,
    norm_gain,
    expert_ids,
    gate_values,
    gate_proj,
    up_proj,
    down_proj,
):
    req_count = lax.axis_size("req")
    kv_count = lax.axis_size("kv")
    req_index = lax.axis_index("req")
    kv_index = lax.axis_index("kv")
    per_dev = residual_in.shape[0]
    head_dim = fresh_token_keys.shape[1]
    col_count = residual_in.shape[1]
    total_reqs = lengths.shape[0]
    model_width = out_proj.shape[1]
    q_width = queries.shape[1]

    pieces = (queries, fresh_token_keys, fresh_token_values, residual_in)
    slot_of = jnp.zeros((total_reqs,), jnp.int32).at[slot_order].set(
        jnp.arange(total_reqs, dtype=jnp.int32)
    )
    slots_grid = slot_order.reshape(req_count, per_dev)
    from_grid = slots_grid % per_dev
    sent_here = (slots_grid // per_dev == req_index)[:, :, None]

    def to_slot_rows(piece):
        rows = jnp.broadcast_to(piece[0], (req_count, per_dev, piece.shape[1]))
        for i in range(1, per_dev):
            rows = jnp.where((from_grid == i)[:, :, None], piece[i][None, None, :], rows)
        return jnp.where(sent_here, rows, jnp.zeros((), piece.dtype))

    to_slots = jnp.concatenate([to_slot_rows(piece) for piece in pieces], axis=2)
    from_homes = lax.all_to_all(to_slots, "req", 0, 0, tiled=False)
    served = lax.dynamic_slice_in_dim(slot_order, req_index * per_dev, per_dev)
    mine = from_homes[served // per_dev, jnp.arange(per_dev)]
    query_rows = mine[:, :q_width].reshape(per_dev, -1, head_dim)
    self_key_row = mine[:, q_width:q_width + head_dim]
    self_value_row = mine[:, q_width + head_dim:q_width + 2 * head_dim]
    residual_rows = mine[:, q_width + 2 * head_dim:]
    live_len = lengths[served]

    inv_root = 1.0 / math.sqrt(head_dim)
    scores = (
        jnp.einsum("rqd,rld->rql", query_rows, cached_key_slots, preferred_element_type=jnp.float32)
        * inv_root
    )
    positions = jnp.arange(cached_key_slots.shape[1])
    scores = jnp.where((positions[None, :] < live_len[:, None])[:, None, :], scores, -1e30)
    own_score = (
        jnp.einsum("rqd,rd->rq", query_rows, self_key_row, preferred_element_type=jnp.float32)
        * inv_root
    )
    highest = jnp.maximum(jnp.max(scores, axis=2), own_score)
    weights = jnp.exp(scores - highest[:, :, None])
    own_weight = jnp.exp(own_score - highest)
    totals = jnp.sum(weights, axis=2) + own_weight
    numerator = jnp.einsum(
        "rql,rld->rqd",
        weights.astype(jnp.bfloat16),
        cached_value_slots,
        preferred_element_type=jnp.float32,
    )
    own_low = lax.optimization_barrier(own_weight.astype(jnp.bfloat16)).astype(jnp.float32)
    numerator = numerator + own_low[:, :, None] * self_value_row.astype(jnp.float32)[:, None, :]
    attended = (numerator / totals[:, :, None]).astype(jnp.bfloat16).reshape(per_dev, -1)
    projected = jnp.dot(attended, out_proj, preferred_element_type=jnp.float32)

    col_start = kv_index * col_count
    summed_in = projected + lax.dynamic_update_slice(
        jnp.zeros((per_dev, model_width), jnp.float32),
        residual_rows.astype(jnp.float32),
        (0, col_start),
    )
    far_last = sorted(range(1, kv_count), key=lambda shift: min(shift, kv_count - shift))
    far_first = far_last[::-1]
    sent_rows = {
        shift: lax.ppermute(
            summed_in, "kv", [(i, (i + shift) % kv_count) for i in range(kv_count)]
        )
        for shift in far_first
    }
    parts = [summed_in] + [sent_rows[shift] for shift in far_last]
    summed = parts[0]
    for part in parts[1:]:
        summed = summed + part
    hidden = summed
    squares = jnp.sum(hidden * hidden, axis=1)
    own_hidden = lax.dynamic_slice_in_dim(hidden, col_start, col_count, axis=1)
    normed = (
        own_hidden
        * lax.rsqrt(squares / model_width + 1e-06)[:, None]
        * norm_gain.astype(jnp.float32)[None, :]
    ).astype(jnp.bfloat16)
    local_count = gate_proj.shape[0]
    served_ids = expert_ids[served] // local_count
    wanted = jnp.any(
        served_ids[None, :, :] == jnp.arange(req_count, dtype=jnp.int32)[:, None, None], axis=2
    )
    to_experts = jnp.where(wanted[:, :, None], normed[None, :, :], jnp.zeros_like(normed)[None])
    by_slot = lax.all_to_all(to_experts, "req", 0, 0, tiled=False)

    capacity = min(2 * total_reqs * expert_ids.shape[1] // (local_count * req_count), total_reqs)
    expert = req_index * local_count + 0
    named_here = expert_ids == expert
    token_gate = jnp.sum(jnp.where(named_here, gate_values, 0.0), axis=1)
    uses_expert = jnp.any(named_here, axis=1)
    picked = jnp.nonzero(uses_expert, size=capacity, fill_value=0)[0].astype(jnp.int32)
    valid_rows = jnp.arange(capacity) < jnp.sum(uses_expert.astype(jnp.int32))
    picked_slots = slot_of[picked]
    row_block = by_slot[picked_slots // per_dev, picked_slots % per_dev]
    peer_rows_of = {
        shift: lax.ppermute(row_block, "kv", [(i, (i + shift) % kv_count) for i in range(kv_count)])
        for shift in far_first
    }
    kv_shifts = far_last
    from_peers = [peer_rows_of[shift] for shift in kv_shifts]

    def block_rows(weights, source):
        return lax.dynamic_slice_in_dim(weights, source * col_count, col_count, axis=0)

    gate_h = jnp.dot(row_block, block_rows(gate_proj[0], kv_index), preferred_element_type=jnp.float32)
    up_h = jnp.dot(row_block, block_rows(up_proj[0], kv_index), preferred_element_type=jnp.float32)
    for shift, peer_rows in zip(kv_shifts, from_peers):
        source = (kv_index - shift) % kv_count
        gate_h = gate_h + jnp.dot(
            peer_rows, block_rows(gate_proj[0], source), preferred_element_type=jnp.float32
        )
        up_h = up_h + jnp.dot(
            peer_rows, block_rows(up_proj[0], source), preferred_element_type=jnp.float32
        )
    inner_act = (jax.nn.silu(gate_h) * up_h).astype(jnp.bfloat16)
    row_gate = jnp.where(valid_rows, token_gate[picked], 0.0)

    def down_block(block):
        cols = lax.dynamic_slice_in_dim(down_proj[0], block * col_count, col_count, axis=1)
        return jnp.dot(inner_act, cols, preferred_element_type=jnp.float32) * row_gate[:, None]

    sent = [
        lax.ppermute(
            down_block((kv_index + shift) % kv_count),
            "kv",
            [(i, (i + shift) % kv_count) for i in range(kv_count)],
        )
        for shift in far_first
    ]
    weighted = down_block(kv_index) + sum(sent[::-1])

    at_pick = jnp.where(uses_expert, jnp.cumsum(uses_expert.astype(jnp.int32)) - 1, capacity)
    weighted_ext = jnp.concatenate([weighted, jnp.zeros((1, col_count), jnp.float32)], axis=0)
    halves = []
    for j in range(per_dev):
        home_slot = slot_of[j::per_dev]
        own_row = own_hidden[0][None, :]
        for i in range(1, per_dev):
            own_row = jnp.where((home_slot % per_dev == i)[:, None], own_hidden[i][None, :], own_row)
        halves.append(
            weighted_ext[at_pick[j::per_dev]]
            + jnp.where((home_slot // per_dev == req_index)[:, None], own_row, 0.0)
        )
    combined = jnp.stack(halves, axis=1).astype(jnp.bfloat16)
    layer_rows = jnp.sum(
        lax.all_to_all(combined, "req", 0, 0, tiled=False).astype(jnp.float32), axis=0
    )
    return layer_rows.astype(jnp.bfloat16)


def solution(mesh):
    in_specs = (
        P("req", "kv"),
        P("req", "kv"),
        P("req", "kv"),
        P("req", "kv"),
        P("req", None, "kv"),
        P("req", None, "kv"),
        P(),
        P(),
        P("kv", None),
        P("kv"),
        P(),
        P(),
        P("req", None, "kv"),
        P("req", None, "kv"),
        P("req", "kv", None),
    )
    out_specs = P("req", "kv")
    return jax.shard_map(
        per_device, mesh=mesh, in_specs=in_specs, out_specs=out_specs, check_vma=False
    )
```

```python
import math

import jax
import jax.numpy as jnp
from jax import lax
from jax.sharding import PartitionSpec as P


def per_device(
    residual_in,
    queries,
    fresh_token_keys,
    fresh_token_values,
    cached_key_slots,
    cached_value_slots,
    lengths,
    slot_order,
    out_proj,
    norm_gain,
    expert_ids,
    gate_values,
    gate_proj,
    up_proj,
    down_proj,
):
    req_count = lax.axis_size("req")
    kv_count = lax.axis_size("kv")
    req_index = lax.axis_index("req")
    kv_index = lax.axis_index("kv")
    per_dev = residual_in.shape[0]
    head_dim = fresh_token_keys.shape[1]
    col_count = residual_in.shape[1]
    total_reqs = lengths.shape[0]
    model_width = out_proj.shape[1]
    q_width = queries.shape[1]

    pieces = (queries, fresh_token_keys, fresh_token_values, residual_in)
    slot_of = jnp.zeros((total_reqs,), jnp.int32).at[slot_order].set(
        jnp.arange(total_reqs, dtype=jnp.int32)
    )
    slots_grid = slot_order.reshape(req_count, per_dev)
    from_grid = slots_grid % per_dev
    sent_here = (slots_grid // per_dev == req_index)[:, :, None]

    def to_slot_rows(piece):
        rows = jnp.broadcast_to(piece[0], (req_count, per_dev, piece.shape[1]))
        for i in range(1, per_dev):
            rows = jnp.where((from_grid == i)[:, :, None], piece[i][None, None, :], rows)
        return jnp.where(sent_here, rows, jnp.zeros((), piece.dtype))

    to_slots = jnp.concatenate([to_slot_rows(piece) for piece in pieces], axis=2)
    from_homes = lax.all_to_all(to_slots, "req", 0, 0, tiled=False)
    served = lax.dynamic_slice_in_dim(slot_order, req_index * per_dev, per_dev)
    mine = jnp.concatenate(
        [
            lax.dynamic_slice(
                from_homes, (served[j] // per_dev, j, 0), (1, 1, from_homes.shape[2])
            )[0]
            for j in range(per_dev)
        ],
        axis=0,
    )
    query_rows = mine[:, :q_width].reshape(per_dev, -1, head_dim)
    self_key_row = mine[:, q_width:q_width + head_dim]
    self_value_row = mine[:, q_width + head_dim:q_width + 2 * head_dim]
    residual_rows = mine[:, q_width + 2 * head_dim:]
    live_len = lengths[served]

    inv_root = 1.0 / math.sqrt(head_dim)
    scores = (
        jnp.einsum("rqd,rld->rql", query_rows, cached_key_slots, preferred_element_type=jnp.float32)
        * inv_root
    )
    positions = jnp.arange(cached_key_slots.shape[1])
    scores = jnp.where((positions[None, :] < live_len[:, None])[:, None, :], scores, -1e30)
    own_score = (
        jnp.einsum("rqd,rd->rq", query_rows, self_key_row, preferred_element_type=jnp.float32)
        * inv_root
    )
    highest = jnp.maximum(jnp.max(scores, axis=2), own_score)
    weights = jnp.exp(scores - highest[:, :, None])
    own_weight = jnp.exp(own_score - highest)
    totals = jnp.sum(weights, axis=2) + own_weight
    numerator = jnp.einsum(
        "rql,rld->rqd",
        weights.astype(jnp.bfloat16),
        cached_value_slots,
        preferred_element_type=jnp.float32,
    )
    own_low = lax.optimization_barrier(own_weight.astype(jnp.bfloat16)).astype(jnp.float32)
    numerator = numerator + own_low[:, :, None] * self_value_row.astype(jnp.float32)[:, None, :]
    attended = (numerator / totals[:, :, None]).astype(jnp.bfloat16).reshape(per_dev, -1)
    projected = jnp.dot(attended, out_proj, preferred_element_type=jnp.float32)

    col_start = kv_index * col_count
    summed_in = projected + lax.dynamic_update_slice(
        jnp.zeros((per_dev, model_width), jnp.float32),
        residual_rows.astype(jnp.float32),
        (0, col_start),
    )
    parts = [summed_in] + [
        lax.ppermute(summed_in, "kv", [(i, (i + shift) % kv_count) for i in range(kv_count)])
        for shift in range(1, kv_count)
    ]
    summed = parts[0]
    for part in parts[1:]:
        summed = summed + part
    hidden = summed
    squares = jnp.sum(hidden * hidden, axis=1)
    own_hidden = lax.dynamic_slice_in_dim(hidden, col_start, col_count, axis=1)
    normed = (
        own_hidden
        * lax.rsqrt(squares / model_width + 1e-06)[:, None]
        * norm_gain.astype(jnp.float32)[None, :]
    ).astype(jnp.bfloat16)
    local_count = gate_proj.shape[0]
    served_ids = expert_ids[served] // local_count
    wanted = jnp.any(
        served_ids[None, :, :] == jnp.arange(req_count, dtype=jnp.int32)[:, None, None], axis=2
    )
    to_experts = jnp.where(wanted[:, :, None], normed[None, :, :], jnp.zeros_like(normed)[None])
    by_slot = lax.all_to_all(to_experts, "req", 0, 0, tiled=False)

    capacity = min(2 * total_reqs * expert_ids.shape[1] // (local_count * req_count), total_reqs)
    expert = req_index * local_count + 0
    named_here = expert_ids == expert
    token_gate = jnp.sum(jnp.where(named_here, gate_values, 0.0), axis=1)
    uses_expert = jnp.any(named_here, axis=1)
    picked = jnp.nonzero(uses_expert, size=capacity, fill_value=0)[0].astype(jnp.int32)
    valid_rows = jnp.arange(capacity) < jnp.sum(uses_expert.astype(jnp.int32))
    picked_slots = slot_of[picked]
    row_block = by_slot[picked_slots // per_dev, picked_slots % per_dev]
    kv_shifts = range(1, kv_count)
    from_peers = [
        lax.ppermute(row_block, "kv", [(i, (i + shift) % kv_count) for i in range(kv_count)])
        for shift in kv_shifts
    ]

    def block_rows(weights, source):
        return lax.dynamic_slice_in_dim(weights, source * col_count, col_count, axis=0)

    gate_h = jnp.dot(row_block, block_rows(gate_proj[0], kv_index), preferred_element_type=jnp.float32)
    up_h = jnp.dot(row_block, block_rows(up_proj[0], kv_index), preferred_element_type=jnp.float32)
    for shift, peer_rows in zip(kv_shifts, from_peers):
        source = (kv_index - shift) % kv_count
        gate_h = gate_h + jnp.dot(
            peer_rows, block_rows(gate_proj[0], source), preferred_element_type=jnp.float32
        )
        up_h = up_h + jnp.dot(
            peer_rows, block_rows(up_proj[0], source), preferred_element_type=jnp.float32
        )
    inner_act = (jax.nn.silu(gate_h) * up_h).astype(jnp.bfloat16)
    row_gate = jnp.where(valid_rows, token_gate[picked], 0.0)

    def down_block(block):
        cols = lax.dynamic_slice_in_dim(down_proj[0], block * col_count, col_count, axis=1)
        return jnp.dot(inner_act, cols, preferred_element_type=jnp.float32) * row_gate[:, None]

    sent = [
        lax.ppermute(
            down_block((kv_index + shift) % kv_count),
            "kv",
            [(i, (i + shift) % kv_count) for i in range(kv_count)],
        )
        for shift in range(1, kv_count)
    ]
    weighted = down_block(kv_index) + sum(sent)

    at_pick = jnp.where(uses_expert, jnp.cumsum(uses_expert.astype(jnp.int32)) - 1, capacity)
    weighted_ext = jnp.concatenate([weighted, jnp.zeros((1, col_count), jnp.float32)], axis=0)
    halves = []
    for j in range(per_dev):
        home_slot = slot_of[j::per_dev]
        own_row = own_hidden[0][None, :]
        for i in range(1, per_dev):
            own_row = jnp.where((home_slot % per_dev == i)[:, None], own_hidden[i][None, :], own_row)
        halves.append(
            weighted_ext[at_pick[j::per_dev]]
            + jnp.where((home_slot // per_dev == req_index)[:, None], own_row, 0.0)
        )
    combined = jnp.stack(halves, axis=1).astype(jnp.bfloat16)
    layer_rows = jnp.sum(
        lax.all_to_all(combined, "req", 0, 0, tiled=False).astype(jnp.float32), axis=0
    )
    return layer_rows.astype(jnp.bfloat16)


def solution(mesh):
    in_specs = (
        P("req", "kv"),
        P("req", "kv"),
        P("req", "kv"),
        P("req", "kv"),
        P("req", None, "kv"),
        P("req", None, "kv"),
        P(),
        P(),
        P("kv", None),
        P("kv"),
        P(),
        P(),
        P("req", None, "kv"),
        P("req", None, "kv"),
        P("req", "kv", None),
    )
    out_specs = P("req", "kv")
    return jax.shard_map(
        per_device, mesh=mesh, in_specs=in_specs, out_specs=out_specs, check_vma=False
    )
```
